32 devices in a mesh: shots: 2 (over y), gx: 4 (over z), gy: 4 (over x, core).
Axes of the slice: x: 2, y: 2, z: 4, core: 2. Of those that a mesh axis runs over, the one named last changes fastest.
Arguments:
- p_now: float32 [64, 64, 128], P(('shots', 'gx'), 'gy'), parts along dimension 0, may hold values from -6 to 6
- q_now: float32 [64, 64, 128], P(('shots', 'gx'), 'gy'), parts along dimension 0, may hold values from -6 to 6
- p_prev: float32 [64, 64, 128], P(('shots', 'gx'), 'gy'), parts along dimension 0, may hold values from -6 to 6
- q_prev: float32 [64, 64, 128], P(('shots', 'gx'), 'gy'), parts along dimension 0, may hold values from -6 to 6
- speed: float32 [32, 64, 128], P('gx', 'gy'), may hold values from 0.05 to 0.2
- epsilon: float32 [32, 64, 128], P('gx', 'gy'), may hold values from 0.05 to 0.35
- delta: float32 [32, 64, 128], P('gx', 'gy'), may hold values from 0 to 0.3
- theta: float32 [32, 64, 128], P('gx', 'gy'), may hold values from -1 to 1
- phi: float32 [32, 64, 128], P('gx', 'gy'), may hold values from -3.140625 to 3.140625
- snapshots: bfloat16 [2, 64, 64, 128], P(None, ('shots', 'gx'), 'gy'), parts along dimension 1, may hold values from -6 to 6
- traces: float32 [1024, 4096], P(None, ('shots', 'gx', 'gy')), parts along dimension 1, may hold values from -6 to 6
- time_steps: int32 [4], P('shots'), parts along dimension 0, may hold values from 0 to 1023
- rec_owner: int32 [4096, 1], P(('shots', 'gx', 'gy')), parts along dimension 0, may hold values from 0 to 3; in each aligned block of 128 rows (0 to 127, 128 to 255, ...) at most 64 rows name the same one
- rec_local: int32 [4096], P(('shots', 'gx', 'gy')), parts along dimension 0, may hold values from 0 to 16383
Outputs:
- p_next: float32 [64, 64, 128], P(('shots', 'gx'), 'gy'), parts along dimension 0
- q_next: float32 [64, 64, 128], P(('shots', 'gx'), 'gy'), parts along dimension 0
- p_mid: float32 [64, 64, 128], P(('shots', 'gx'), 'gy'), parts along dimension 0
- q_mid: float32 [64, 64, 128], P(('shots', 'gx'), 'gy'), parts along dimension 0
- image: float32 [64, 64, 128], P(('shots', 'gx'), 'gy'), parts along dimension 0
The draws below stay inside these ranges and needn't reach their ends.
There are 2 independent parts, one for each index of `shots`. The reference program is written for one: setup_inputs(seed, part) draws one part's arguments, and reference() takes and returns one part's arrays. A program takes and returns all parts, laid end to end along the dimension named above; an argument that names none is the same for every part. Nothing has to cross between parts.
Inputs may be any that keep to these rules, and one draw needn't show every extreme that they name: `rec_owner`: the 128 receivers of one device (aligned blocks of 128 rows) name any one owner at most 64 times, a bound that some block reaches. `rec_local`: A receiver's cell lies in the band of the second dimension that the device holding the receiver covers.
All inputs are finite; a program needn't handle non-finite values.
Results may differ from the reference program's by a relative error of at most 0.0003.
Values sent between devices are 32-bit elements; how exact they have to be, the bound alone decides.
No kernel may reach another device: no remote copies, remote signals or barrier semaphores. Data moves between devices by JAX's collectives and lax.ppermute only.
A program may use at most 64 MiB of HBM per device.

```python
import math
import jax
import jax.numpy as jnp
import numpy as np

CX = 8
CY = 16
CZ = 128
R_DEV = 128
NT = 1024
CAP = 64
NX = 32
NY = 64
NZ = 128
RECV = 2048
N_GX = 4
N_GY = 4


def plant(array, own_key, smallest, largest):
    longest = array.shape.index(max(array.shape))
    spots = []
    for shift in (0, 1):
        where = [jax.random.randint(jax.random.fold_in(own_key, axis), (), 0, length) for axis, length in enumerate(array.shape)]
        where[longest] = (where[longest] + shift) % array.shape[longest]
        spots.append(tuple(where))
    return array.at[spots[0]].set(smallest).at[spots[1]].set(largest)


def levels(stream_key, extent, split, low, high):
    loudness, own = 1.0, jax.random.fold_in(stream_key, 6)
    for axis_at, shards_of in split:
        draws = jnp.exp(jax.random.uniform(jax.random.fold_in(own, axis_at), (shards_of,), jnp.float32, low / len(split), high / len(split)))
        loudness = loudness * jnp.repeat(draws, extent[axis_at] // shards_of).reshape([-1 if axis == axis_at else 1 for axis in range(len(extent))])
    return loudness


def shared_out(rng, own, number, rows, count, top, limit, lean):
    order = jax.random.permutation(rng, count)
    crowded, ordinary = load_shares(count, rows * top, limit, lean, True), load_shares(count, rows * top, limit, lean, False)
    places = jnp.arange(count)

    def named(lengths, offset_by):
        used = int((lengths > 0).sum())
        fixed = max(1, used // 4)
        shifted = fixed + (places - fixed + offset_by * (used - fixed)) % max(1, count - fixed)
        return jnp.zeros((count,), jnp.int32).at[order[jnp.where(places < fixed, places, shifted)]].set(jnp.asarray(lengths, jnp.int32))

    lengths = jnp.where(number % 4 == 0, named(crowded, number // 4), named(ordinary, number - number // 4 - 1))
    mixed = jax.random.permutation(jax.random.fold_in(own, 3), count)
    donor, sink = mixed[0:count // 2 * 2:2], mixed[1:count // 2 * 2:2]
    margin = jnp.minimum(lengths[donor] - 1, limit - lengths[sink]) // 2
    margin = jnp.where((donor == order[0]) | (sink == order[0]) | (lengths[sink] == 0), 0, jnp.maximum(margin, 0))
    shifted = jax.random.randint(jax.random.fold_in(own, 4), (count // 2,), 0, 1 << 20) % (margin + 1)
    lengths = lengths.at[donor].add(-shifted).at[sink].add(shifted)
    members = jnp.searchsorted(jnp.cumsum(lengths), jnp.arange(rows * top), side="right").astype(jnp.int32)
    listing = members.reshape(top, rows).T
    listing = listing[jax.random.permutation(jax.random.fold_in(own, 1), rows)]
    offset_by = jax.random.randint(jax.random.fold_in(own, 2), (rows, 1), 0, top)
    return jnp.take_along_axis(listing, (jnp.arange(top)[None, :] + offset_by) % top, axis=1)


def load_shares(number_of, total, most, slope, full):
    weights = [(1 << 20) // math.isqrt(grade ** slope) + 1 for grade in range(1, number_of + 1)]
    largest = most if full else min(most, max(-(-total // number_of), total * weights[0] // sum(weights)))
    least = 1 if total - largest >= number_of - 1 else 0
    given, rest = [largest] + [least] * (number_of - 1), total - largest - least * (number_of - 1)
    while rest > 0:
        free = [i for i in range(1, number_of) if given[i] < largest] or [i for i in range(1, number_of) if given[i] < most]
        whole, budget = sum([weights[i] for i in free]), rest
        for i in free:
            more = min(most - given[i], max(1, budget * weights[i] // whole), rest)
            given[i] = given[i] + more
            rest = rest - more
    return np.array(given)


def scatter_about(own_key, dims, scale, reach, split=(), kind=jnp.bfloat16):
    values = scale * jax.random.normal(own_key, dims, jnp.float32)
    if split:
        values = values * levels(own_key, dims, split, -0.22, 0.18)
    return jnp.clip(values, -reach, reach).astype(kind)


def setup_inputs(seed: int = 0, part: int = 0) -> dict:
    keys = jax.random.split(jax.random.key(seed), 15)
    part_keys = jax.random.split(jax.random.fold_in(keys[14], part), 15)
    p_now = scatter_about(part_keys[0], (NX, NY, NZ), 1.0, 6.0, ((0, 4), (1, 4)), jnp.float32)
    q_now = scatter_about(part_keys[1], (NX, NY, NZ), 1.0, 6.0, ((0, 4), (1, 4)), jnp.float32)
    p_prev = scatter_about(part_keys[2], (NX, NY, NZ), 1.0, 6.0, ((0, 4), (1, 4)), jnp.float32)
    q_prev = scatter_about(part_keys[3], (NX, NY, NZ), 1.0, 6.0, ((0, 4), (1, 4)), jnp.float32)
    speed = jnp.clip(jnp.exp(math.log(0.2) - 1.3862944 * jax.random.uniform(keys[4], (NX, NY, NZ), jnp.float32) ** levels(keys[4], (NX, NY, NZ), ((0, 4), (1, 4)), -0.2, 0.2)), 0.05, 0.2)
    epsilon = jnp.clip(0.05 + 0.29999999 * jax.random.uniform(keys[5], (NX, NY, NZ), jnp.float32) ** levels(keys[5], (NX, NY, NZ), ((0, 4), (1, 4)), -0.2, 0.2), 0.05, 0.35)
    delta = jnp.clip(0.3 * jax.random.uniform(keys[6], (NX, NY, NZ), jnp.float32) ** levels(keys[6], (NX, NY, NZ), ((0, 4), (1, 4)), -0.2, 0.2), 0.0, 0.3)
    theta = jnp.clip(jax.random.uniform(keys[7], (NX, NY, NZ), jnp.float32, -1.0, 1.0) * levels(keys[7], (NX, NY, NZ), ((0, 4), (1, 4)), -0.4, 0.0), -1.0, 1.0)
    phi = jnp.clip(jax.random.uniform(keys[8], (NX, NY, NZ), jnp.float32, -3.140625, 3.140625), -3.140625, 3.140625)
    snapshots = scatter_about(part_keys[9], (2, NX, NY, NZ), 1.0, 6.0, ((1, 4), (2, 4)))
    traces = scatter_about(part_keys[10], (NT, RECV), 1.0, 6.0, ((1, 16),), jnp.float32)
    time_steps = jax.random.randint(part_keys[11], (2,), 0, NT).astype(jnp.int32)
    rec_owner_keys = jax.random.split(jax.random.fold_in(part_keys[12], 1), RECV // R_DEV)
    rec_owner_turns = jax.random.permutation(jax.random.fold_in(part_keys[12], 3), RECV // R_DEV)
    rec_owner = jax.vmap(lambda own, number: shared_out(jax.random.fold_in(part_keys[12], 2), own, number, R_DEV, N_GX, 1, CAP, 2))(rec_owner_keys, rec_owner_turns).reshape((RECV, 1))
    rec_local = plant(jax.random.randint(part_keys[13], (RECV,), 0, CX * CY * CZ), jax.random.fold_in(part_keys[13], 1), 0, (CX * CY * CZ) - 1).astype(jnp.int32)
    return {"p_now": p_now, "q_now": q_now, "p_prev": p_prev, "q_prev": q_prev, "speed": speed, "epsilon": epsilon, "delta": delta, "theta": theta, "phi": phi, "snapshots": snapshots, "traces": traces, "time_steps": time_steps, "rec_owner": rec_owner, "rec_local": rec_local}


second_coef = (-205.0 / 72.0, 8.0 / 5.0, -1.0 / 5.0, 8.0 / 315.0, -1.0 / 560.0)
first_coef = (4.0 / 5.0, -1.0 / 5.0, 4.0 / 105.0, -1.0 / 280.0)

def derivatives(padded, sx, sy, sz):

    def part(dx, dy, dz):
        return padded[:, 4 + dx:4 + dx + sx, 4 + dy:4 + dy + sy, 4 + dz:4 + dz + sz]
    centre = part(0, 0, 0)
    dxx = second_coef[0] * centre
    dyy = second_coef[0] * centre
    dzz = second_coef[0] * centre
    for k in range(1, 5):
        dxx = dxx + second_coef[k] * (part(k, 0, 0) + part(-k, 0, 0))
        dyy = dyy + second_coef[k] * (part(0, k, 0) + part(0, -k, 0))
        dzz = dzz + second_coef[k] * (part(0, 0, k) + part(0, 0, -k))
    dy_wide = 0.0
    dz_xwide = 0.0
    dz_ywide = 0.0
    for k in range(1, 5):
        weight = first_coef[k - 1]
        dy_wide = dy_wide + weight * (padded[:, :, 4 + k:4 + k + sy, 4:4 + sz] - padded[:, :, 4 - k:4 - k + sy, 4:4 + sz])
        dz_xwide = dz_xwide + weight * (padded[:, :, 4:4 + sy, 4 + k:4 + k + sz] - padded[:, :, 4:4 + sy, 4 - k:4 - k + sz])
        dz_ywide = dz_ywide + weight * (padded[:, 4:4 + sx, :, 4 + k:4 + k + sz] - padded[:, 4:4 + sx, :, 4 - k:4 - k + sz])
    dxy = 0.0
    dxz = 0.0
    dyz = 0.0
    for k in range(1, 5):
        weight = first_coef[k - 1]
        dxy = dxy + weight * (dy_wide[:, 4 + k:4 + k + sx] - dy_wide[:, 4 - k:4 - k + sx])
        dxz = dxz + weight * (dz_xwide[:, 4 + k:4 + k + sx] - dz_xwide[:, 4 - k:4 - k + sx])
        dyz = dyz + weight * (dz_ywide[:, :, 4 + k:4 + k + sy] - dz_ywide[:, :, 4 - k:4 - k + sy])
    return (centre, dxx, dyy, dzz, dxy, dxz, dyz)

def advance(padded, previous, speed, epsilon, delta, theta, phi, source):
    sx, sy, sz = (previous.shape[1], previous.shape[2], previous.shape[3])
    centre, dxx, dyy, dzz, dxy, dxz, dyz = derivatives(padded, sx, sy, sz)
    axis_x = jnp.sin(theta) * jnp.cos(phi)
    axis_y = jnp.sin(theta) * jnp.sin(phi)
    axis_z = jnp.cos(theta)
    rotated = axis_x * axis_x * dxx + axis_y * axis_y * dyy + axis_z * axis_z * dzz + 2.0 * axis_x * axis_y * dxy + 2.0 * axis_x * axis_z * dxz + 2.0 * axis_y * axis_z * dyz
    remainder = dxx + dyy + dzz - rotated
    root_delta = jnp.sqrt(1.0 + 2.0 * delta)
    p_new = 2.0 * centre[0] - previous[0] + speed * ((1.0 + 2.0 * epsilon) * remainder[0] + root_delta * rotated[1]) + source
    q_new = 2.0 * centre[1] - previous[1] + speed * (root_delta * remainder[0] + rotated[1]) + source
    return jnp.stack([p_new, q_new])

def pad_all(fields):
    return jnp.pad(fields, ((0, 0), (4, 4), (4, 4), (4, 4)))

def reference(p_now, q_now, p_prev, q_prev, speed, epsilon, delta, theta, phi, snapshots, traces, time_steps, rec_owner, rec_local):
    receiver = jnp.arange(RECV, dtype=jnp.int32)
    band = receiver // R_DEV % N_GY
    first = rec_owner[:, 0] * CX + rec_local // (CY * CZ)
    second = band * CY + rec_local // CZ % CY
    third = rec_local % CZ
    flat = (first * NY + second) * NZ + third
    samples = jnp.take(traces, time_steps, axis=0)
    sources = jnp.zeros((2, NX * NY * NZ), jnp.float32).at[:, flat].add(samples)
    sources = sources.reshape(2, NX, NY, NZ)
    current = jnp.stack([p_now, q_now])
    earlier = jnp.stack([p_prev, q_prev])
    middle = advance(pad_all(current), earlier, speed, epsilon, delta, theta, phi, sources[0])
    final = advance(pad_all(middle), current, speed, epsilon, delta, theta, phi, sources[1])
    image = snapshots[0].astype(jnp.float32) * middle[0] + snapshots[1].astype(jnp.float32) * final[0]
    return (final[0], final[1], middle[0], middle[1], image)
```

```python
import jax
import jax.numpy as jnp
from jax import lax
from jax.sharding import PartitionSpec as P

second_coef = (-205.0 / 72.0, 8.0 / 5.0, -1.0 / 5.0, 8.0 / 315.0, -1.0 / 560.0)
first_coef = (4.0 / 5.0, -1.0 / 5.0, 4.0 / 105.0, -1.0 / 280.0)


def padded_2(cells, sides, width):
    for axis, dim in sides:
        count = lax.axis_size(axis)
        ends = count - 1
        head = lax.slice_in_dim(cells, 0, width, axis=dim)
        tail = lax.slice_in_dim(cells, cells.shape[dim] - width, cells.shape[dim], axis=dim)
        cells = jnp.concatenate(
            [
                lax.ppermute(tail, axis, [(i, (i + 1) % count) for i in range(ends)]),
                cells,
                lax.ppermute(head, axis, [((i + 1) % count, i) for i in range(ends)]),
            ],
            axis=dim,
        )
    return cells


def derivatives(padded, sx, sy, sz):

    def part(dx, dy, dz):
        return padded[:, 4 + dx : 4 + dx + sx, 4 + dy : 4 + dy + sy, 4 + dz : 4 + dz + sz]

    centre = part(0, 0, 0)
    dxx = second_coef[0] * centre
    dyy = second_coef[0] * centre
    dzz = second_coef[0] * centre
    for k in range(1, 5):
        dxx = dxx + second_coef[k] * (part(k, 0, 0) + part(-k, 0, 0))
        dyy = dyy + second_coef[k] * (part(0, k, 0) + part(0, -k, 0))
        dzz = dzz + second_coef[k] * (part(0, 0, k) + part(0, 0, -k))
    dy_wide = 0.0
    dz_xwide = 0.0
    dz_ywide = 0.0
    for k in range(1, 5):
        weight = first_coef[k - 1]
        dy_wide = dy_wide + weight * (
            padded[:, :, 4 + k : 4 + k + sy, 4 : 4 + sz]
            - padded[:, :, 4 - k : 4 - k + sy, 4 : 4 + sz]
        )
        dz_xwide = dz_xwide + weight * (
            padded[:, :, 4 : 4 + sy, 4 + k : 4 + k + sz]
            - padded[:, :, 4 : 4 + sy, 4 - k : 4 - k + sz]
        )
        dz_ywide = dz_ywide + weight * (
            padded[:, 4 : 4 + sx, :, 4 + k : 4 + k + sz]
            - padded[:, 4 : 4 + sx, :, 4 - k : 4 - k + sz]
        )
    dxy = 0.0
    dxz = 0.0
    dyz = 0.0
    for k in range(1, 5):
        weight = first_coef[k - 1]
        dxy = dxy + weight * (dy_wide[:, 4 + k : 4 + k + sx] - dy_wide[:, 4 - k : 4 - k + sx])
        dxz = dxz + weight * (dz_xwide[:, 4 + k : 4 + k + sx] - dz_xwide[:, 4 - k : 4 - k + sx])
        dyz = dyz + weight * (
            dz_ywide[:, :, 4 + k : 4 + k + sy] - dz_ywide[:, :, 4 - k : 4 - k + sy]
        )
    return (centre, dxx, dyy, dzz, dxy, dxz, dyz)


def advance(padded, previous, speed, epsilon, delta, theta, phi, source):
    sx, sy, sz = (previous.shape[1], previous.shape[2], previous.shape[3])
    centre, dxx, dyy, dzz, dxy, dxz, dyz = derivatives(padded, sx, sy, sz)
    axis_x = jnp.sin(theta) * jnp.cos(phi)
    axis_y = jnp.sin(theta) * jnp.sin(phi)
    axis_z = jnp.cos(theta)
    rotated = (
        axis_x * axis_x * dxx
        + axis_y * axis_y * dyy
        + axis_z * axis_z * dzz
        + 2.0 * axis_x * axis_y * dxy
        + 2.0 * axis_x * axis_z * dxz
        + 2.0 * axis_y * axis_z * dyz
    )
    remainder = dxx + dyy + dzz - rotated
    root_delta = jnp.sqrt(1.0 + 2.0 * delta)
    p_new = (
        2.0 * centre[0]
        - previous[0]
        + speed * ((1.0 + 2.0 * epsilon) * remainder[0] + root_delta * rotated[1])
        + source
    )
    q_new = (
        2.0 * centre[1] - previous[1] + speed * (root_delta * remainder[0] + rotated[1]) + source
    )
    return jnp.stack([p_new, q_new])


def pad_depth(fields):
    return jnp.pad(fields, ((0, 0), (0, 0), (0, 0), (4, 4)))


def widened(fields):
    return pad_depth(padded_2(fields, (("gx", 1), ("gy", 2)), 4))


def receiver_sources(traces, time_steps, rec_owner, rec_local, shape):
    sx, sy, sz = shape
    groups = lax.axis_size("gx")
    held = rec_local.shape[0]
    samples = [lax.dynamic_index_in_dim(traces, time_steps[k], 0, keepdims=False) for k in range(2)]
    payload = jnp.stack(
        samples + [rec_local.astype(jnp.float32), rec_owner[:, 0].astype(jnp.float32)]
    )
    sent = jnp.broadcast_to(payload[None], (groups, 4, held))
    arrived = lax.all_to_all(sent, "gx", split_axis=0, concat_axis=0, tiled=True)
    arrived = jnp.transpose(arrived, (1, 0, 2)).reshape(4, groups * held)
    mine = arrived[3].astype(jnp.int32) == lax.axis_index("gx")
    cell = arrived[2].astype(jnp.int32)
    plane = cell // sz
    depth = cell % sz
    values = jnp.where(mine[None, :], arrived[0:2], 0.0)
    picks = (plane[None, :] == jnp.arange(sx * sy, dtype=jnp.int32)[:, None]).astype(jnp.float32)
    spread = values[:, None, :] * picks[None, :, :]
    columns = (depth[:, None] == jnp.arange(sz, dtype=jnp.int32)[None, :]).astype(jnp.float32)
    sources = jnp.einsum(
        "cpr,rz->cpz", spread, columns, precision=lax.Precision.HIGHEST,
        preferred_element_type=jnp.float32,
    )
    return sources.reshape(2, sx, sy, sz)


def local(
    p_now,
    q_now,
    p_prev,
    q_prev,
    speed,
    epsilon,
    delta,
    theta,
    phi,
    snapshots,
    traces,
    time_steps,
    rec_owner,
    rec_local,
):
    sources = receiver_sources(traces, time_steps, rec_owner, rec_local, p_now.shape)
    current = jnp.stack([p_now, q_now])
    earlier = jnp.stack([p_prev, q_prev])
    middle = advance(widened(current), earlier, speed, epsilon, delta, theta, phi, sources[0])
    final = advance(widened(middle), current, speed, epsilon, delta, theta, phi, sources[1])
    image = (
        snapshots[0].astype(jnp.float32) * middle[0] + snapshots[1].astype(jnp.float32) * final[0]
    )
    return (final[0], final[1], middle[0], middle[1], image)


def solution(mesh):
    return jax.shard_map(
        local,
        mesh=mesh,
        in_specs=(
            P(("shots", "gx"), "gy", None),
            P(("shots", "gx"), "gy", None),
            P(("shots", "gx"), "gy", None),
            P(("shots", "gx"), "gy", None),
            P("gx", "gy", None),
            P("gx", "gy", None),
            P("gx", "gy", None),
            P("gx", "gy", None),
            P("gx", "gy", None),
            P(None, ("shots", "gx"), "gy", None),
            P(None, ("shots", "gx", "gy")),
            P("shots"),
            P(("shots", "gx", "gy"), None),
            P(("shots", "gx", "gy")),
        ),
        out_specs=(
            P(("shots", "gx"), "gy", None),
            P(("shots", "gx"), "gy", None),
            P(("shots", "gx"), "gy", None),
            P(("shots", "gx"), "gy", None),
            P(("shots", "gx"), "gy", None),
        ),
        check_vma=False,
    )
```

```python
import jax
import jax.numpy as jnp
from jax import lax
from jax.sharding import PartitionSpec as P

second_coef = (-205.0 / 72.0, 8.0 / 5.0, -1.0 / 5.0, 8.0 / 315.0, -1.0 / 560.0)
first_coef = (4.0 / 5.0, -1.0 / 5.0, 4.0 / 105.0, -1.0 / 280.0)


def padded_2(cells, sides, width):
    for axis, dim in sides:
        count = lax.axis_size(axis)
        ends = count - 1
        head = lax.slice_in_dim(cells, 0, width, axis=dim)
        tail = lax.slice_in_dim(cells, cells.shape[dim] - width, cells.shape[dim], axis=dim)
        cells = jnp.concatenate(
            [
                lax.ppermute(tail, axis, [(i, (i + 1) % count) for i in range(ends)]),
                cells,
                lax.ppermute(head, axis, [((i + 1) % count, i) for i in range(ends)]),
            ],
            axis=dim,
        )
    return cells


def derivatives(padded, sx, sy, sz):

    def part(dx, dy, dz):
        return padded[:, 4 + dx : 4 + dx + sx, 4 + dy : 4 + dy + sy, 4 + dz : 4 + dz + sz]

    centre = part(0, 0, 0)
    dxx = second_coef[0] * centre
    dyy = second_coef[0] * centre
    dzz = second_coef[0] * centre
    for k in range(1, 5):
        dxx = dxx + second_coef[k] * (part(k, 0, 0) + part(-k, 0, 0))
        dyy = dyy + second_coef[k] * (part(0, k, 0) + part(0, -k, 0))
        dzz = dzz + second_coef[k] * (part(0, 0, k) + part(0, 0, -k))
    dy_wide = 0.0
    dz_xwide = 0.0
    dz_ywide = 0.0
    for k in range(1, 5):
        weight = first_coef[k - 1]
        dy_wide = dy_wide + weight * (
            padded[:, :, 4 + k : 4 + k + sy, 4 : 4 + sz]
            - padded[:, :, 4 - k : 4 - k + sy, 4 : 4 + sz]
        )
        dz_xwide = dz_xwide + weight * (
            padded[:, :, 4 : 4 + sy, 4 + k : 4 + k + sz]
            - padded[:, :, 4 : 4 + sy, 4 - k : 4 - k + sz]
        )
        dz_ywide = dz_ywide + weight * (
            padded[:, 4 : 4 + sx, :, 4 + k : 4 + k + sz]
            - padded[:, 4 : 4 + sx, :, 4 - k : 4 - k + sz]
        )
    dxy = 0.0
    dxz = 0.0
    dyz = 0.0
    for k in range(1, 5):
        weight = first_coef[k - 1]
        dxy = dxy + weight * (dy_wide[:, 4 + k : 4 + k + sx] - dy_wide[:, 4 - k : 4 - k + sx])
        dxz = dxz + weight * (dz_xwide[:, 4 + k : 4 + k + sx] - dz_xwide[:, 4 - k : 4 - k + sx])
        dyz = dyz + weight * (
            dz_ywide[:, :, 4 + k : 4 + k + sy] - dz_ywide[:, :, 4 - k : 4 - k + sy]
        )
    return (centre, dxx, dyy, dzz, dxy, dxz, dyz)


def advance(padded, previous, speed, epsilon, delta, theta, phi, source):
    sx, sy, sz = (previous.shape[1], previous.shape[2], previous.shape[3])
    centre, dxx, dyy, dzz, dxy, dxz, dyz = derivatives(padded, sx, sy, sz)
    axis_x = jnp.sin(theta) * jnp.cos(phi)
    axis_y = jnp.sin(theta) * jnp.sin(phi)
    axis_z = jnp.cos(theta)
    rotated = (
        axis_x * axis_x * dxx
        + axis_y * axis_y * dyy
        + axis_z * axis_z * dzz
        + 2.0 * axis_x * axis_y * dxy
        + 2.0 * axis_x * axis_z * dxz
        + 2.0 * axis_y * axis_z * dyz
    )
    remainder = dxx + dyy + dzz - rotated
    root_delta = jnp.sqrt(1.0 + 2.0 * delta)
    p_new = (
        2.0 * centre[0]
        - previous[0]
        + speed * ((1.0 + 2.0 * epsilon) * remainder[0] + root_delta * rotated[1])
        + source
    )
    q_new = (
        2.0 * centre[1] - previous[1] + speed * (root_delta * remainder[0] + rotated[1]) + source
    )
    return jnp.stack([p_new, q_new])


def pad_depth(fields):
    return jnp.pad(fields, ((0, 0), (0, 0), (0, 0), (4, 4)))


def widened(fields):
    return pad_depth(padded_2(fields, (("gx", 1), ("gy", 2)), 4))


def receiver_sources(traces, time_steps, rec_owner, rec_local, shape):
    sx, sy, sz = shape
    groups = lax.axis_size("gx")
    held = rec_local.shape[0]
    samples = [lax.dynamic_index_in_dim(traces, time_steps[k], 0, keepdims=False) for k in range(2)]
    payload = jnp.stack(
        samples + [rec_local.astype(jnp.float32), rec_owner[:, 0].astype(jnp.float32)]
    )
    if groups & (groups - 1) == 0:
        arrived = payload
        step = 1
        while step < groups:
            partner = lax.ppermute(arrived, "gx", [(i, i ^ step) for i in range(groups)])
            arrived = jnp.concatenate([arrived, partner], axis=1)
            step *= 2
    else:
        sent = jnp.broadcast_to(payload[None], (groups, 4, held))
        arrived = lax.all_to_all(sent, "gx", split_axis=0, concat_axis=0, tiled=True)
        arrived = jnp.transpose(arrived, (1, 0, 2)).reshape(4, groups * held)
    mine = arrived[3].astype(jnp.int32) == lax.axis_index("gx")
    cell = arrived[2].astype(jnp.int32)
    plane = cell // sz
    depth = cell % sz
    values = jnp.where(mine[None, :], arrived[0:2], 0.0)
    picks = (plane[None, :] == jnp.arange(sx * sy, dtype=jnp.int32)[:, None]).astype(jnp.float32)
    spread = values[:, None, :] * picks[None, :, :]
    columns = (depth[:, None] == jnp.arange(sz, dtype=jnp.int32)[None, :]).astype(jnp.float32)
    sources = jnp.einsum(
        "cpr,rz->cpz", spread, columns, precision=lax.Precision.HIGHEST,
        preferred_element_type=jnp.float32,
    )
    return sources.reshape(2, sx, sy, sz)


def local(
    p_now,
    q_now,
    p_prev,
    q_prev,
    speed,
    epsilon,
    delta,
    theta,
    phi,
    snapshots,
    traces,
    time_steps,
    rec_owner,
    rec_local,
):
    sources = receiver_sources(traces, time_steps, rec_owner, rec_local, p_now.shape)
    current = jnp.stack([p_now, q_now])
    earlier = jnp.stack([p_prev, q_prev])
    middle = advance(widened(current), earlier, speed, epsilon, delta, theta, phi, sources[0])
    final = advance(widened(middle), current, speed, epsilon, delta, theta, phi, sources[1])
    image = (
        snapshots[0].astype(jnp.float32) * middle[0] + snapshots[1].astype(jnp.float32) * final[0]
    )
    return (final[0], final[1], middle[0], middle[1], image)


def solution(mesh):
    return jax.shard_map(
        local,
        mesh=mesh,
        in_specs=(
            P(("shots", "gx"), "gy", None),
            P(("shots", "gx"), "gy", None),
            P(("shots", "gx"), "gy", None),
            P(("shots", "gx"), "gy", None),
            P("gx", "gy", None),
            P("gx", "gy", None),
            P("gx", "gy", None),
            P("gx", "gy", None),
            P("gx", "gy", None),
            P(None, ("shots", "gx"), "gy", None),
            P(None, ("shots", "gx", "gy")),
            P("shots"),
            P(("shots", "gx", "gy"), None),
            P(("shots", "gx", "gy")),
        ),
        out_specs=(
            P(("shots", "gx"), "gy", None),
            P(("shots", "gx"), "gy", None),
            P(("shots", "gx"), "gy", None),
            P(("shots", "gx"), "gy", None),
            P(("shots", "gx"), "gy", None),
        ),
        check_vma=False,
    )
```

```python
import jax
import jax.numpy as jnp
from jax import lax
from jax.sharding import PartitionSpec as P

second_coef = (-205.0 / 72.0, 8.0 / 5.0, -1.0 / 5.0, 8.0 / 315.0, -1.0 / 560.0)
first_coef = (4.0 / 5.0, -1.0 / 5.0, 4.0 / 105.0, -1.0 / 280.0)


def padded_2(cells, sides, width):
    for axis, dim in sides:
        count = lax.axis_size(axis)
        ends = count - 1
        head = lax.slice_in_dim(cells, 0, width, axis=dim)
        tail = lax.slice_in_dim(cells, cells.shape[dim] - width, cells.shape[dim], axis=dim)
        cells = jnp.concatenate(
            [
                lax.ppermute(tail, axis, [(i, (i + 1) % count) for i in range(ends)]),
                cells,
                lax.ppermute(head, axis, [((i + 1) % count, i) for i in range(ends)]),
            ],
            axis=dim,
        )
    return cells


def derivatives(padded, sx, sy, sz):

    def part(dx, dy, dz):
        return padded[:, 4 + dx : 4 + dx + sx, 4 + dy : 4 + dy + sy, 4 + dz : 4 + dz + sz]

    centre = part(0, 0, 0)
    dxx = second_coef[0] * centre
    dyy = second_coef[0] * centre
    dzz = second_coef[0] * centre
    for k in range(1, 5):
        dxx = dxx + second_coef[k] * (part(k, 0, 0) + part(-k, 0, 0))
        dyy = dyy + second_coef[k] * (part(0, k, 0) + part(0, -k, 0))
        dzz = dzz + second_coef[k] * (part(0, 0, k) + part(0, 0, -k))
    dy_wide = 0.0
    dz_xwide = 0.0
    dz_ywide = 0.0
    for k in range(1, 5):
        weight = first_coef[k - 1]
        dy_wide = dy_wide + weight * (
            padded[:, :, 4 + k : 4 + k + sy, 4 : 4 + sz]
            - padded[:, :, 4 - k : 4 - k + sy, 4 : 4 + sz]
        )
        dz_xwide = dz_xwide + weight * (
            padded[:, :, 4 : 4 + sy, 4 + k : 4 + k + sz]
            - padded[:, :, 4 : 4 + sy, 4 - k : 4 - k + sz]
        )
        dz_ywide = dz_ywide + weight * (
            padded[:, 4 : 4 + sx, :, 4 + k : 4 + k + sz]
            - padded[:, 4 : 4 + sx, :, 4 - k : 4 - k + sz]
        )
    dxy = 0.0
    dxz = 0.0
    dyz = 0.0
    for k in range(1, 5):
        weight = first_coef[k - 1]
        dxy = dxy + weight * (dy_wide[:, 4 + k : 4 + k + sx] - dy_wide[:, 4 - k : 4 - k + sx])
        dxz = dxz + weight * (dz_xwide[:, 4 + k : 4 + k + sx] - dz_xwide[:, 4 - k : 4 - k + sx])
        dyz = dyz + weight * (
            dz_ywide[:, :, 4 + k : 4 + k + sy] - dz_ywide[:, :, 4 - k : 4 - k + sy]
        )
    return (centre, dxx, dyy, dzz, dxy, dxz, dyz)


def advance(padded, previous, speed, epsilon, delta, theta, phi, source):
    sx, sy, sz = (previous.shape[1], previous.shape[2], previous.shape[3])
    centre, dxx, dyy, dzz, dxy, dxz, dyz = derivatives(padded, sx, sy, sz)
    axis_x = jnp.sin(theta) * jnp.cos(phi)
    axis_y = jnp.sin(theta) * jnp.sin(phi)
    axis_z = jnp.cos(theta)
    rotated = (
        axis_x * axis_x * dxx
        + axis_y * axis_y * dyy
        + axis_z * axis_z * dzz
        + 2.0 * axis_x * axis_y * dxy
        + 2.0 * axis_x * axis_z * dxz
        + 2.0 * axis_y * axis_z * dyz
    )
    remainder = dxx + dyy + dzz - rotated
    root_delta = jnp.sqrt(1.0 + 2.0 * delta)
    p_new = (
        2.0 * centre[0]
        - previous[0]
        + speed * ((1.0 + 2.0 * epsilon) * remainder[0] + root_delta * rotated[1])
        + source
    )
    q_new = (
        2.0 * centre[1] - previous[1] + speed * (root_delta * remainder[0] + rotated[1]) + source
    )
    return jnp.stack([p_new, q_new])


def pad_depth(fields):
    return jnp.pad(fields, ((0, 0), (0, 0), (0, 0), (4, 4)))


def from_neighbours(low_part, high_part, axis):
    count = lax.axis_size(axis)
    below = lax.ppermute(low_part, axis, [(i, i + 1) for i in range(count - 1)])
    above = lax.ppermute(high_part, axis, [(i + 1, i) for i in range(count - 1)])
    return below, above


def gather_column(traces, time_steps, rec_owner, rec_local):
    groups = lax.axis_size("gx")
    held = rec_local.shape[0]
    samples = [lax.dynamic_index_in_dim(traces, time_steps[k], 0, keepdims=False) for k in range(2)]
    payload = jnp.stack(
        samples + [rec_local.astype(jnp.float32), rec_owner[:, 0].astype(jnp.float32)]
    )
    if groups & (groups - 1) == 0:
        arrived = payload
        step = 1
        while step < groups:
            partner = lax.ppermute(arrived, "gx", [(i, i ^ step) for i in range(groups)])
            arrived = jnp.concatenate([arrived, partner], axis=1)
            step *= 2
        return arrived
    sent = jnp.broadcast_to(payload[None], (groups, 4, held))
    arrived = lax.all_to_all(sent, "gx", split_axis=0, concat_axis=0, tiled=True)
    return jnp.transpose(arrived, (1, 0, 2)).reshape(4, groups * held)


def sources_over(arrived, values, shape, first, rows):
    sx, sy, sz = shape
    cell = arrived[2].astype(jnp.int32)
    owner = arrived[3].astype(jnp.int32)
    row = (owner - lax.axis_index("gx")) * sx + cell // (sy * sz) - first
    inside = (row >= 0) & (row < rows)
    plane = jnp.where(inside, row * sy + cell // sz % sy, -1)
    depth = cell % sz
    picks = (plane[None, :] == jnp.arange(rows * sy, dtype=jnp.int32)[:, None]).astype(jnp.float32)
    spread = values[:, None, :] * picks[None, :, :]
    columns = (depth[:, None] == jnp.arange(sz, dtype=jnp.int32)[None, :]).astype(jnp.float32)
    sources = jnp.einsum(
        "cpr,rz->cpz", spread, columns, precision=lax.Precision.HIGHEST,
        preferred_element_type=jnp.float32,
    )
    return sources.reshape(values.shape[0], rows, sy, sz)


def local(
    p_now,
    q_now,
    p_prev,
    q_prev,
    speed,
    epsilon,
    delta,
    theta,
    phi,
    snapshots,
    traces,
    time_steps,
    rec_owner,
    rec_local,
):
    sx, sy, sz = p_now.shape
    assert sx >= 8
    current = jnp.stack([p_now, q_now])
    earlier = jnp.stack([p_prev, q_prev])
    params = jnp.stack([speed, epsilon, delta, theta, phi])
    def slabs(parts):
        return jnp.concatenate([part.reshape(-1, sy, sz) for part in parts], axis=0)

    low_part = slabs([current[:, sx - 8 :], earlier[:, sx - 4 :], params[:, sx - 4 :]])
    high_part = slabs([current[:, :8], earlier[:, :4], params[:, :4]])
    below, above = from_neighbours(low_part, high_part, "gx")

    def unpack(got):
        return (
            got[0:16].reshape(2, 8, sy, sz),
            got[16:24].reshape(2, 4, sy, sz),
            got[24:44].reshape(5, 4, sy, sz),
        )

    (now_lo, prev_lo, params_lo), (now_hi, prev_hi, params_hi) = unpack(below), unpack(above)
    now_x = jnp.concatenate([now_lo, current, now_hi], axis=1)
    prev_x = jnp.concatenate([prev_lo, earlier, prev_hi], axis=1)
    params_x = jnp.concatenate([params_lo, params, params_hi], axis=1)
    lo_y, hi_y = from_neighbours(now_x[:, :, sy - 4 :], now_x[:, :, :4], "gy")
    now_xy = pad_depth(jnp.concatenate([lo_y, now_x, hi_y], axis=2))

    arrived = gather_column(traces, time_steps, rec_owner, rec_local)
    source_0 = sources_over(arrived, arrived[0:1], (sx, sy, sz), -4, sx + 8)[0]
    source_1 = sources_over(arrived, arrived[1:2], (sx, sy, sz), 0, sx)[0]

    mid_x = advance(now_xy, prev_x, *params_x, source_0)
    middle = mid_x[:, 4 : 4 + sx]
    lo_m, hi_m = from_neighbours(mid_x[:, :, sy - 4 :], mid_x[:, :, :4], "gy")
    mid_xy = pad_depth(jnp.concatenate([lo_m, mid_x, hi_m], axis=2))
    final = advance(mid_xy, current, speed, epsilon, delta, theta, phi, source_1)
    image = (
        snapshots[0].astype(jnp.float32) * middle[0] + snapshots[1].astype(jnp.float32) * final[0]
    )
    return (final[0], final[1], middle[0], middle[1], image)


def solution(mesh):
    return jax.shard_map(
        local,
        mesh=mesh,
        in_specs=(
            P(("shots", "gx"), "gy", None),
            P(("shots", "gx"), "gy", None),
            P(("shots", "gx"), "gy", None),
            P(("shots", "gx"), "gy", None),
            P("gx", "gy", None),
            P("gx", "gy", None),
            P("gx", "gy", None),
            P("gx", "gy", None),
            P("gx", "gy", None),
            P(None, ("shots", "gx"), "gy", None),
            P(None, ("shots", "gx", "gy")),
            P("shots"),
            P(("shots", "gx", "gy"), None),
            P(("shots", "gx", "gy")),
        ),
        out_specs=(
            P(("shots", "gx"), "gy", None),
            P(("shots", "gx"), "gy", None),
            P(("shots", "gx"), "gy", None),
            P(("shots", "gx"), "gy", None),
            P(("shots", "gx"), "gy", None),
        ),
        check_vma=False,
    )
```

```python
import jax
import jax.numpy as jnp
from jax import lax
from jax.sharding import PartitionSpec as P

second_coef = (-205.0 / 72.0, 8.0 / 5.0, -1.0 / 5.0, 8.0 / 315.0, -1.0 / 560.0)
first_coef = (4.0 / 5.0, -1.0 / 5.0, 4.0 / 105.0, -1.0 / 280.0)


def padded_2(cells, sides, width):
    for axis, dim in sides:
        count = lax.axis_size(axis)
        ends = count - 1
        head = lax.slice_in_dim(cells, 0, width, axis=dim)
        tail = lax.slice_in_dim(cells, cells.shape[dim] - width, cells.shape[dim], axis=dim)
        cells = jnp.concatenate(
            [
                lax.ppermute(tail, axis, [(i, (i + 1) % count) for i in range(ends)]),
                cells,
                lax.ppermute(head, axis, [((i + 1) % count, i) for i in range(ends)]),
            ],
            axis=dim,
        )
    return cells


def derivatives(padded, sx, sy, sz):

    def part(dx, dy, dz):
        return padded[:, 4 + dx : 4 + dx + sx, 4 + dy : 4 + dy + sy, 4 + dz : 4 + dz + sz]

    centre = part(0, 0, 0)
    dxx = second_coef[0] * centre
    dyy = second_coef[0] * centre
    dzz = second_coef[0] * centre
    for k in range(1, 5):
        dxx = dxx + second_coef[k] * (part(k, 0, 0) + part(-k, 0, 0))
        dyy = dyy + second_coef[k] * (part(0, k, 0) + part(0, -k, 0))
        dzz = dzz + second_coef[k] * (part(0, 0, k) + part(0, 0, -k))
    dy_wide = 0.0
    dz_xwide = 0.0
    dz_ywide = 0.0
    for k in range(1, 5):
        weight = first_coef[k - 1]
        dy_wide = dy_wide + weight * (
            padded[:, :, 4 + k : 4 + k + sy, 4 : 4 + sz]
            - padded[:, :, 4 - k : 4 - k + sy, 4 : 4 + sz]
        )
        dz_xwide = dz_xwide + weight * (
            padded[:, :, 4 : 4 + sy, 4 + k : 4 + k + sz]
            - padded[:, :, 4 : 4 + sy, 4 - k : 4 - k + sz]
        )
        dz_ywide = dz_ywide + weight * (
            padded[:, 4 : 4 + sx, :, 4 + k : 4 + k + sz]
            - padded[:, 4 : 4 + sx, :, 4 - k : 4 - k + sz]
        )
    dxy = 0.0
    dxz = 0.0
    dyz = 0.0
    for k in range(1, 5):
        weight = first_coef[k - 1]
        dxy = dxy + weight * (dy_wide[:, 4 + k : 4 + k + sx] - dy_wide[:, 4 - k : 4 - k + sx])
        dxz = dxz + weight * (dz_xwide[:, 4 + k : 4 + k + sx] - dz_xwide[:, 4 - k : 4 - k + sx])
        dyz = dyz + weight * (
            dz_ywide[:, :, 4 + k : 4 + k + sy] - dz_ywide[:, :, 4 - k : 4 - k + sy]
        )
    return (centre, dxx, dyy, dzz, dxy, dxz, dyz)


def advance(padded, previous, speed, epsilon, delta, theta, phi, source):
    sx, sy, sz = (previous.shape[1], previous.shape[2], previous.shape[3])
    centre, dxx, dyy, dzz, dxy, dxz, dyz = derivatives(padded, sx, sy, sz)
    axis_x = jnp.sin(theta) * jnp.cos(phi)
    axis_y = jnp.sin(theta) * jnp.sin(phi)
    axis_z = jnp.cos(theta)
    rotated = (
        axis_x * axis_x * dxx
        + axis_y * axis_y * dyy
        + axis_z * axis_z * dzz
        + 2.0 * axis_x * axis_y * dxy
        + 2.0 * axis_x * axis_z * dxz
        + 2.0 * axis_y * axis_z * dyz
    )
    remainder = dxx + dyy + dzz - rotated
    root_delta = jnp.sqrt(1.0 + 2.0 * delta)
    p_new = (
        2.0 * centre[0]
        - previous[0]
        + speed * ((1.0 + 2.0 * epsilon) * remainder[0] + root_delta * rotated[1])
        + source
    )
    q_new = (
        2.0 * centre[1] - previous[1] + speed * (root_delta * remainder[0] + rotated[1]) + source
    )
    return jnp.stack([p_new, q_new])


def pad_depth(fields):
    return jnp.pad(fields, ((0, 0), (0, 0), (0, 0), (4, 4)))


def from_neighbours(low_part, high_part, axis):
    count = lax.axis_size(axis)
    below = lax.ppermute(low_part, axis, [(i, i + 1) for i in range(count - 1)])
    above = lax.ppermute(high_part, axis, [(i + 1, i) for i in range(count - 1)])
    return below, above


def gather_column(traces, time_steps, rec_owner, rec_local):
    groups = lax.axis_size("gx")
    held = rec_local.shape[0]
    steps = jnp.arange(traces.shape[0], dtype=jnp.int32)
    chosen = (time_steps[:, None] == steps[None, :]).astype(jnp.float32)
    samples = jnp.dot(
        chosen, traces, precision=lax.Precision.HIGHEST, preferred_element_type=jnp.float32
    )
    payload = jnp.concatenate(
        [samples, rec_local.astype(jnp.float32)[None], rec_owner[:, 0].astype(jnp.float32)[None]]
    )
    if groups & (groups - 1) == 0:
        arrived = payload
        step = 1
        while step < groups:
            partner = lax.ppermute(arrived, "gx", [(i, i ^ step) for i in range(groups)])
            arrived = jnp.concatenate([arrived, partner], axis=1)
            step *= 2
        return arrived
    sent = jnp.broadcast_to(payload[None], (groups, 4, held))
    arrived = lax.all_to_all(sent, "gx", split_axis=0, concat_axis=0, tiled=True)
    return jnp.transpose(arrived, (1, 0, 2)).reshape(4, groups * held)


def sources_over(arrived, values, shape, first, rows):
    sx, sy, sz = shape
    cell = arrived[2].astype(jnp.int32)
    owner = arrived[3].astype(jnp.int32)
    row = (owner - lax.axis_index("gx")) * sx + cell // (sy * sz) - first
    inside = (row >= 0) & (row < rows)
    plane = jnp.where(inside, row * sy + cell // sz % sy, -1)
    depth = cell % sz
    picks = (plane[None, :] == jnp.arange(rows * sy, dtype=jnp.int32)[:, None]).astype(jnp.float32)
    spread = values[:, None, :] * picks[None, :, :]
    columns = (depth[:, None] == jnp.arange(sz, dtype=jnp.int32)[None, :]).astype(jnp.float32)
    sources = jnp.einsum(
        "cpr,rz->cpz", spread, columns, precision=lax.Precision.HIGHEST,
        preferred_element_type=jnp.float32,
    )
    return sources.reshape(values.shape[0], rows, sy, sz)


def local(
    p_now,
    q_now,
    p_prev,
    q_prev,
    speed,
    epsilon,
    delta,
    theta,
    phi,
    snapshots,
    traces,
    time_steps,
    rec_owner,
    rec_local,
):
    sx, sy, sz = p_now.shape
    assert sx == 8
    current = jnp.stack([p_now, q_now])
    earlier = jnp.stack([p_prev, q_prev])
    params = (speed, epsilon, delta, theta, phi)

    def slabs(parts):
        return jnp.concatenate([part.reshape(-1, sy, sz) for part in parts], axis=0)

    low_part = slabs(
        [p_now, q_now, p_prev[sx - 4 :], q_prev[sx - 4 :]] + [f[sx - 4 :] for f in params]
    )
    high_part = slabs([p_now, q_now, p_prev[:4], q_prev[:4]] + [f[:4] for f in params])
    below, above = from_neighbours(low_part, high_part, "gx")

    def unpack(got):
        return (
            got[0:16].reshape(2, 8, sy, sz),
            got[16:24].reshape(2, 4, sy, sz),
            got[24:44].reshape(5, 4, sy, sz),
        )

    (now_lo, prev_lo, params_lo), (now_hi, prev_hi, params_hi) = unpack(below), unpack(above)
    now_x = jnp.concatenate([now_lo, current, now_hi], axis=1)
    prev_x = jnp.concatenate([prev_lo, earlier, prev_hi], axis=1)
    params_x = [
        jnp.concatenate([params_lo[k], params[k], params_hi[k]], axis=0) for k in range(5)
    ]
    lo_y, hi_y = from_neighbours(now_x[:, :, sy - 4 :], now_x[:, :, :4], "gy")
    now_xy = pad_depth(jnp.concatenate([lo_y, now_x, hi_y], axis=2))

    arrived = gather_column(traces, time_steps, rec_owner, rec_local)
    source_0 = sources_over(arrived, arrived[0:1], (sx, sy, sz), -4, sx + 8)[0]
    source_1 = sources_over(arrived, arrived[1:2], (sx, sy, sz), 0, sx)[0]

    mid_x = advance(now_xy, prev_x, *params_x, source_0)
    middle = mid_x[:, 4 : 4 + sx]
    lo_m, hi_m = from_neighbours(mid_x[:, :, sy - 4 :], mid_x[:, :, :4], "gy")
    mid_xy = pad_depth(jnp.concatenate([lo_m, mid_x, hi_m], axis=2))
    final = advance(mid_xy, current, speed, epsilon, delta, theta, phi, source_1)
    image = (
        snapshots[0].astype(jnp.float32) * middle[0] + snapshots[1].astype(jnp.float32) * final[0]
    )
    return (final[0], final[1], middle[0], middle[1], image)


def solution(mesh):
    return jax.shard_map(
        local,
        mesh=mesh,
        in_specs=(
            P(("shots", "gx"), "gy", None),
            P(("shots", "gx"), "gy", None),
            P(("shots", "gx"), "gy", None),
            P(("shots", "gx"), "gy", None),
            P("gx", "gy", None),
            P("gx", "gy", None),
            P("gx", "gy", None),
            P("gx", "gy", None),
            P("gx", "gy", None),
            P(None, ("shots", "gx"), "gy", None),
            P(None, ("shots", "gx", "gy")),
            P("shots"),
            P(("shots", "gx", "gy"), None),
            P(("shots", "gx", "gy")),
        ),
        out_specs=(
            P(("shots", "gx"), "gy", None),
            P(("shots", "gx"), "gy", None),
            P(("shots", "gx"), "gy", None),
            P(("shots", "gx"), "gy", None),
            P(("shots", "gx"), "gy", None),
        ),
        check_vma=False,
    )
```

```python
import jax
import jax.numpy as jnp
from jax import lax
from jax.sharding import PartitionSpec as P

second_coef = (-205.0 / 72.0, 8.0 / 5.0, -1.0 / 5.0, 8.0 / 315.0, -1.0 / 560.0)
first_coef = (4.0 / 5.0, -1.0 / 5.0, 4.0 / 105.0, -1.0 / 280.0)


def padded_2(cells, sides, width):
    for axis, dim in sides:
        count = lax.axis_size(axis)
        ends = count - 1
        head = lax.slice_in_dim(cells, 0, width, axis=dim)
        tail = lax.slice_in_dim(cells, cells.shape[dim] - width, cells.shape[dim], axis=dim)
        cells = jnp.concatenate(
            [
                lax.ppermute(tail, axis, [(i, (i + 1) % count) for i in range(ends)]),
                cells,
                lax.ppermute(head, axis, [((i + 1) % count, i) for i in range(ends)]),
            ],
            axis=dim,
        )
    return cells


def derivatives(padded, sx, sy, sz):

    def part(dx, dy, dz):
        return padded[:, 4 + dx : 4 + dx + sx, 4 + dy : 4 + dy + sy, 4 + dz : 4 + dz + sz]

    centre = part(0, 0, 0)
    dxx = second_coef[0] * centre
    dyy = second_coef[0] * centre
    dzz = second_coef[0] * centre
    for k in range(1, 5):
        dxx = dxx + second_coef[k] * (part(k, 0, 0) + part(-k, 0, 0))
        dyy = dyy + second_coef[k] * (part(0, k, 0) + part(0, -k, 0))
        dzz = dzz + second_coef[k] * (part(0, 0, k) + part(0, 0, -k))
    dy_wide = 0.0
    dz_xwide = 0.0
    dz_ywide = 0.0
    for k in range(1, 5):
        weight = first_coef[k - 1]
        dy_wide = dy_wide + weight * (
            padded[:, :, 4 + k : 4 + k + sy, 4 : 4 + sz]
            - padded[:, :, 4 - k : 4 - k + sy, 4 : 4 + sz]
        )
        dz_xwide = dz_xwide + weight * (
            padded[:, :, 4 : 4 + sy, 4 + k : 4 + k + sz]
            - padded[:, :, 4 : 4 + sy, 4 - k : 4 - k + sz]
        )
        dz_ywide = dz_ywide + weight * (
            padded[:, 4 : 4 + sx, :, 4 + k : 4 + k + sz]
            - padded[:, 4 : 4 + sx, :, 4 - k : 4 - k + sz]
        )
    dxy = 0.0
    dxz = 0.0
    dyz = 0.0
    for k in range(1, 5):
        weight = first_coef[k - 1]
        dxy = dxy + weight * (dy_wide[:, 4 + k : 4 + k + sx] - dy_wide[:, 4 - k : 4 - k + sx])
        dxz = dxz + weight * (dz_xwide[:, 4 + k : 4 + k + sx] - dz_xwide[:, 4 - k : 4 - k + sx])
        dyz = dyz + weight * (
            dz_ywide[:, :, 4 + k : 4 + k + sy] - dz_ywide[:, :, 4 - k : 4 - k + sy]
        )
    return (centre, dxx, dyy, dzz, dxy, dxz, dyz)


def advance(padded, previous, speed, epsilon, delta, theta, phi, source):
    sx, sy, sz = (previous.shape[1], previous.shape[2], previous.shape[3])
    centre, dxx, dyy, dzz, dxy, dxz, dyz = derivatives(padded, sx, sy, sz)
    axis_x = jnp.sin(theta) * jnp.cos(phi)
    axis_y = jnp.sin(theta) * jnp.sin(phi)
    axis_z = jnp.cos(theta)
    rotated = (
        axis_x * axis_x * dxx
        + axis_y * axis_y * dyy
        + axis_z * axis_z * dzz
        + 2.0 * axis_x * axis_y * dxy
        + 2.0 * axis_x * axis_z * dxz
        + 2.0 * axis_y * axis_z * dyz
    )
    remainder = dxx + dyy + dzz - rotated
    root_delta = jnp.sqrt(1.0 + 2.0 * delta)
    p_new = (
        2.0 * centre[0]
        - previous[0]
        + speed * ((1.0 + 2.0 * epsilon) * remainder[0] + root_delta * rotated[1])
        + source
    )
    q_new = (
        2.0 * centre[1] - previous[1] + speed * (root_delta * remainder[0] + rotated[1]) + source
    )
    return jnp.stack([p_new, q_new])


def pad_depth(fields):
    return jnp.pad(fields, ((0, 0), (0, 0), (0, 0), (4, 4)))


def from_neighbours(low_part, high_part, axis):
    count = lax.axis_size(axis)
    below = lax.ppermute(low_part, axis, [(i, i + 1) for i in range(count - 1)])
    above = lax.ppermute(high_part, axis, [(i + 1, i) for i in range(count - 1)])
    return below, above


def receiver_payload(traces, time_steps, rec_owner, rec_local):
    steps = jnp.arange(traces.shape[0], dtype=jnp.int32)
    chosen = (time_steps[:, None] == steps[None, :]).astype(jnp.float32)
    samples = jnp.dot(
        chosen, traces, precision=lax.Precision.HIGHEST, preferred_element_type=jnp.float32
    )
    return jnp.concatenate(
        [samples, rec_local.astype(jnp.float32)[None], rec_owner[:, 0].astype(jnp.float32)[None]]
    )


def gather_column(payload, below, above):
    groups = lax.axis_size("gx")
    held = payload.shape[1]
    if groups & (groups - 1) == 0 and groups >= 2:
        even = lax.axis_index("gx") % 2 == 0
        arrived = jnp.where(
            even,
            jnp.concatenate([payload, above], axis=1),
            jnp.concatenate([below, payload], axis=1),
        )
        step = 2
        while step < groups:
            partner = lax.ppermute(arrived, "gx", [(i, i ^ step) for i in range(groups)])
            arrived = jnp.concatenate([arrived, partner], axis=1)
            step *= 2
        return arrived
    sent = jnp.broadcast_to(payload[None], (groups, 4, held))
    arrived = lax.all_to_all(sent, "gx", split_axis=0, concat_axis=0, tiled=True)
    return jnp.transpose(arrived, (1, 0, 2)).reshape(4, groups * held)


def sources_over(arrived, values, shape, first, rows):
    sx, sy, sz = shape
    cell = arrived[2].astype(jnp.int32)
    owner = arrived[3].astype(jnp.int32)
    row = (owner - lax.axis_index("gx")) * sx + cell // (sy * sz) - first
    inside = (row >= 0) & (row < rows)
    plane = jnp.where(inside, row * sy + cell // sz % sy, -1)
    depth = cell % sz
    picks = (plane[None, :] == jnp.arange(rows * sy, dtype=jnp.int32)[:, None]).astype(jnp.float32)
    spread = values[:, None, :] * picks[None, :, :]
    columns = (depth[:, None] == jnp.arange(sz, dtype=jnp.int32)[None, :]).astype(jnp.float32)
    sources = jnp.einsum(
        "cpr,rz->cpz", spread, columns, precision=lax.Precision.HIGHEST,
        preferred_element_type=jnp.float32,
    )
    return sources.reshape(values.shape[0], rows, sy, sz)


def local(
    p_now,
    q_now,
    p_prev,
    q_prev,
    speed,
    epsilon,
    delta,
    theta,
    phi,
    snapshots,
    traces,
    time_steps,
    rec_owner,
    rec_local,
):
    sx, sy, sz = p_now.shape
    assert sx == 8
    current = jnp.stack([p_now, q_now])
    earlier = jnp.stack([p_prev, q_prev])
    params = (speed, epsilon, delta, theta, phi)

    def slabs(parts):
        return jnp.concatenate([part.reshape(-1, sy, sz) for part in parts], axis=0)

    payload = receiver_payload(traces, time_steps, rec_owner, rec_local)
    held = payload.shape[1]
    extra = -(-4 * held // (sy * sz))
    riding = jnp.pad(payload.reshape(-1), (0, extra * sy * sz - 4 * held)).reshape(extra, sy, sz)
    low_part = slabs(
        [p_now, q_now, p_prev[sx - 4 :], q_prev[sx - 4 :]] + [f[sx - 4 :] for f in params]
        + [riding]
    )
    high_part = slabs(
        [p_now, q_now, p_prev[:4], q_prev[:4]] + [f[:4] for f in params] + [riding]
    )
    below, above = from_neighbours(low_part, high_part, "gx")

    def unpack(got):
        return (
            got[0:16].reshape(2, 8, sy, sz),
            got[16:24].reshape(2, 4, sy, sz),
            got[24:44].reshape(5, 4, sy, sz),
            got[44:].reshape(-1)[: 4 * held].reshape(4, held),
        )

    (now_lo, prev_lo, params_lo, rec_lo), (now_hi, prev_hi, params_hi, rec_hi) = (
        unpack(below),
        unpack(above),
    )
    now_x = jnp.concatenate([now_lo, current, now_hi], axis=1)
    prev_x = jnp.concatenate([prev_lo, earlier, prev_hi], axis=1)
    params_x = [
        jnp.concatenate([params_lo[k], params[k], params_hi[k]], axis=0) for k in range(5)
    ]
    lo_y, hi_y = from_neighbours(now_x[:, :, sy - 4 :], now_x[:, :, :4], "gy")
    now_xy = pad_depth(jnp.concatenate([lo_y, now_x, hi_y], axis=2))

    arrived = gather_column(payload, rec_lo, rec_hi)
    source_0 = sources_over(arrived, arrived[0:1], (sx, sy, sz), -4, sx + 8)[0]
    source_1 = sources_over(arrived, arrived[1:2], (sx, sy, sz), 0, sx)[0]

    mid_x = advance(now_xy, prev_x, *params_x, source_0)
    middle = mid_x[:, 4 : 4 + sx]
    lo_m, hi_m = from_neighbours(mid_x[:, :, sy - 4 :], mid_x[:, :, :4], "gy")
    mid_xy = pad_depth(jnp.concatenate([lo_m, mid_x, hi_m], axis=2))
    final = advance(mid_xy, current, speed, epsilon, delta, theta, phi, source_1)
    image = (
        snapshots[0].astype(jnp.float32) * middle[0] + snapshots[1].astype(jnp.float32) * final[0]
    )
    return (final[0], final[1], middle[0], middle[1], image)


def solution(mesh):
    return jax.shard_map(
        local,
        mesh=mesh,
        in_specs=(
            P(("shots", "gx"), "gy", None),
            P(("shots", "gx"), "gy", None),
            P(("shots", "gx"), "gy", None),
            P(("shots", "gx"), "gy", None),
            P("gx", "gy", None),
            P("gx", "gy", None),
            P("gx", "gy", None),
            P("gx", "gy", None),
            P("gx", "gy", None),
            P(None, ("shots", "gx"), "gy", None),
            P(None, ("shots", "gx", "gy")),
            P("shots"),
            P(("shots", "gx", "gy"), None),
            P(("shots", "gx", "gy")),
        ),
        out_specs=(
            P(("shots", "gx"), "gy", None),
            P(("shots", "gx"), "gy", None),
            P(("shots", "gx"), "gy", None),
            P(("shots", "gx"), "gy", None),
            P(("shots", "gx"), "gy", None),
        ),
        check_vma=False,
    )
```

```python
import jax
import jax.numpy as jnp
from jax import lax
from jax.sharding import PartitionSpec as P

second_coef = (-205.0 / 72.0, 8.0 / 5.0, -1.0 / 5.0, 8.0 / 315.0, -1.0 / 560.0)
first_coef = (4.0 / 5.0, -1.0 / 5.0, 4.0 / 105.0, -1.0 / 280.0)


def padded_2(cells, sides, width):
    for axis, dim in sides:
        count = lax.axis_size(axis)
        ends = count - 1
        head = lax.slice_in_dim(cells, 0, width, axis=dim)
        tail = lax.slice_in_dim(cells, cells.shape[dim] - width, cells.shape[dim], axis=dim)
        cells = jnp.concatenate(
            [
                lax.ppermute(tail, axis, [(i, (i + 1) % count) for i in range(ends)]),
                cells,
                lax.ppermute(head, axis, [((i + 1) % count, i) for i in range(ends)]),
            ],
            axis=dim,
        )
    return cells


def derivatives(padded, sx, sy, sz):

    def part(dx, dy, dz):
        return padded[:, 4 + dx : 4 + dx + sx, 4 + dy : 4 + dy + sy, 4 + dz : 4 + dz + sz]

    centre = part(0, 0, 0)
    dxx = second_coef[0] * centre
    dyy = second_coef[0] * centre
    dzz = second_coef[0] * centre
    for k in range(1, 5):
        dxx = dxx + second_coef[k] * (part(k, 0, 0) + part(-k, 0, 0))
        dyy = dyy + second_coef[k] * (part(0, k, 0) + part(0, -k, 0))
        dzz = dzz + second_coef[k] * (part(0, 0, k) + part(0, 0, -k))
    dy_wide = 0.0
    dz_xwide = 0.0
    dz_ywide = 0.0
    for k in range(1, 5):
        weight = first_coef[k - 1]
        dy_wide = dy_wide + weight * (
            padded[:, :, 4 + k : 4 + k + sy, 4 : 4 + sz]
            - padded[:, :, 4 - k : 4 - k + sy, 4 : 4 + sz]
        )
        dz_xwide = dz_xwide + weight * (
            padded[:, :, 4 : 4 + sy, 4 + k : 4 + k + sz]
            - padded[:, :, 4 : 4 + sy, 4 - k : 4 - k + sz]
        )
        dz_ywide = dz_ywide + weight * (
            padded[:, 4 : 4 + sx, :, 4 + k : 4 + k + sz]
            - padded[:, 4 : 4 + sx, :, 4 - k : 4 - k + sz]
        )
    dxy = 0.0
    dxz = 0.0
    dyz = 0.0
    for k in range(1, 5):
        weight = first_coef[k - 1]
        dxy = dxy + weight * (dy_wide[:, 4 + k : 4 + k + sx] - dy_wide[:, 4 - k : 4 - k + sx])
        dxz = dxz + weight * (dz_xwide[:, 4 + k : 4 + k + sx] - dz_xwide[:, 4 - k : 4 - k + sx])
        dyz = dyz + weight * (
            dz_ywide[:, :, 4 + k : 4 + k + sy] - dz_ywide[:, :, 4 - k : 4 - k + sy]
        )
    return (centre, dxx, dyy, dzz, dxy, dxz, dyz)


def advance(padded, previous, speed, epsilon, delta, theta, phi, source):
    sx, sy, sz = (previous.shape[1], previous.shape[2], previous.shape[3])
    centre, dxx, dyy, dzz, dxy, dxz, dyz = derivatives(padded, sx, sy, sz)
    axis_x = jnp.sin(theta) * jnp.cos(phi)
    axis_y = jnp.sin(theta) * jnp.sin(phi)
    axis_z = jnp.cos(theta)
    rotated = (
        axis_x * axis_x * dxx
        + axis_y * axis_y * dyy
        + axis_z * axis_z * dzz
        + 2.0 * axis_x * axis_y * dxy
        + 2.0 * axis_x * axis_z * dxz
        + 2.0 * axis_y * axis_z * dyz
    )
    remainder = dxx + dyy + dzz - rotated
    root_delta = jnp.sqrt(1.0 + 2.0 * delta)
    p_new = (
        2.0 * centre[0]
        - previous[0]
        + speed * ((1.0 + 2.0 * epsilon) * remainder[0] + root_delta * rotated[1])
        + source
    )
    q_new = (
        2.0 * centre[1] - previous[1] + speed * (root_delta * remainder[0] + rotated[1]) + source
    )
    return jnp.stack([p_new, q_new])


def pad_depth(fields):
    return jnp.pad(fields, ((0, 0), (0, 0), (0, 0), (4, 4)))


def from_neighbours(low_part, high_part, axis):
    count = lax.axis_size(axis)
    below = lax.ppermute(low_part, axis, [(i, i + 1) for i in range(count - 1)])
    above = lax.ppermute(high_part, axis, [(i + 1, i) for i in range(count - 1)])
    return below, above


def gather_column(traces, time_steps, rec_owner, rec_local, after):
    groups = lax.axis_size("gx")
    held = rec_local.shape[0]
    steps = jnp.arange(traces.shape[0], dtype=jnp.int32)
    chosen = (time_steps[:, None] == steps[None, :]).astype(jnp.float32)
    samples = jnp.dot(
        chosen, traces, precision=lax.Precision.HIGHEST, preferred_element_type=jnp.float32
    )
    payload = jnp.concatenate(
        [samples, rec_local.astype(jnp.float32)[None], rec_owner[:, 0].astype(jnp.float32)[None]]
    )
    if groups & (groups - 1) == 0:
        arrived = payload
        step = 1
        while step < groups:
            if step == 2:
                arrived = arrived + 0.0 * after
            partner = lax.ppermute(arrived, "gx", [(i, i ^ step) for i in range(groups)])
            arrived = jnp.concatenate([arrived, partner], axis=1)
            step *= 2
        return arrived
    sent = jnp.broadcast_to(payload[None], (groups, 4, held))
    arrived = lax.all_to_all(sent, "gx", split_axis=0, concat_axis=0, tiled=True)
    return jnp.transpose(arrived, (1, 0, 2)).reshape(4, groups * held)


def sources_over(arrived, values, shape, first, rows):
    sx, sy, sz = shape
    cell = arrived[2].astype(jnp.int32)
    owner = arrived[3].astype(jnp.int32)
    row = (owner - lax.axis_index("gx")) * sx + cell // (sy * sz) - first
    inside = (row >= 0) & (row < rows)
    plane = jnp.where(inside, row * sy + cell // sz % sy, -1)
    depth = cell % sz
    picks = (plane[None, :] == jnp.arange(rows * sy, dtype=jnp.int32)[:, None]).astype(jnp.float32)
    spread = values[:, None, :] * picks[None, :, :]
    columns = (depth[:, None] == jnp.arange(sz, dtype=jnp.int32)[None, :]).astype(jnp.float32)
    sources = jnp.einsum(
        "cpr,rz->cpz", spread, columns, precision=lax.Precision.HIGHEST,
        preferred_element_type=jnp.float32,
    )
    return sources.reshape(values.shape[0], rows, sy, sz)


def local(
    p_now,
    q_now,
    p_prev,
    q_prev,
    speed,
    epsilon,
    delta,
    theta,
    phi,
    snapshots,
    traces,
    time_steps,
    rec_owner,
    rec_local,
):
    sx, sy, sz = p_now.shape
    assert sx == 8
    current = jnp.stack([p_now, q_now])
    earlier = jnp.stack([p_prev, q_prev])
    params = (speed, epsilon, delta, theta, phi)

    def slabs(parts):
        return jnp.concatenate([part.reshape(-1, sy, sz) for part in parts], axis=0)

    low_part = slabs(
        [p_now, q_now, p_prev[sx - 4 :], q_prev[sx - 4 :]] + [f[sx - 4 :] for f in params]
    )
    high_part = slabs([p_now, q_now, p_prev[:4], q_prev[:4]] + [f[:4] for f in params])
    below, above = from_neighbours(low_part, high_part, "gx")

    def unpack(got):
        return (
            got[0:16].reshape(2, 8, sy, sz),
            got[16:24].reshape(2, 4, sy, sz),
            got[24:44].reshape(5, 4, sy, sz),
        )

    (now_lo, prev_lo, params_lo), (now_hi, prev_hi, params_hi) = unpack(below), unpack(above)
    now_x = jnp.concatenate([now_lo, current, now_hi], axis=1)
    prev_x = jnp.concatenate([prev_lo, earlier, prev_hi], axis=1)
    params_x = [
        jnp.concatenate([params_lo[k], params[k], params_hi[k]], axis=0) for k in range(5)
    ]
    lo_y, hi_y = from_neighbours(now_x[:, :, sy - 4 :], now_x[:, :, :4], "gy")
    now_xy = pad_depth(jnp.concatenate([lo_y, now_x, hi_y], axis=2))

    arrived = gather_column(traces, time_steps, rec_owner, rec_local, lo_y[0, 0, 0, 0] + hi_y[0, 0, 0, 0])
    source_0 = sources_over(arrived, arrived[0:1], (sx, sy, sz), -4, sx + 8)[0]
    source_1 = sources_over(arrived, arrived[1:2], (sx, sy, sz), 0, sx)[0]

    mid_x = advance(now_xy, prev_x, *params_x, source_0)
    middle = mid_x[:, 4 : 4 + sx]
    lo_m, hi_m = from_neighbours(mid_x[:, :, sy - 4 :], mid_x[:, :, :4], "gy")
    mid_xy = pad_depth(jnp.concatenate([lo_m, mid_x, hi_m], axis=2))
    final = advance(mid_xy, current, speed, epsilon, delta, theta, phi, source_1)
    image = (
        snapshots[0].astype(jnp.float32) * middle[0] + snapshots[1].astype(jnp.float32) * final[0]
    )
    return (final[0], final[1], middle[0], middle[1], image)


def solution(mesh):
    return jax.shard_map(
        local,
        mesh=mesh,
        in_specs=(
            P(("shots", "gx"), "gy", None),
            P(("shots", "gx"), "gy", None),
            P(("shots", "gx"), "gy", None),
            P(("shots", "gx"), "gy", None),
            P("gx", "gy", None),
            P("gx", "gy", None),
            P("gx", "gy", None),
            P("gx", "gy", None),
            P("gx", "gy", None),
            P(None, ("shots", "gx"), "gy", None),
            P(None, ("shots", "gx", "gy")),
            P("shots"),
            P(("shots", "gx", "gy"), None),
            P(("shots", "gx", "gy")),
        ),
        out_specs=(
            P(("shots", "gx"), "gy", None),
            P(("shots", "gx"), "gy", None),
            P(("shots", "gx"), "gy", None),
            P(("shots", "gx"), "gy", None),
            P(("shots", "gx"), "gy", None),
        ),
        check_vma=False,
    )
```

```python
import jax
import jax.numpy as jnp
from jax import lax
from jax.sharding import PartitionSpec as P

second_coef = (-205.0 / 72.0, 8.0 / 5.0, -1.0 / 5.0, 8.0 / 315.0, -1.0 / 560.0)
first_coef = (4.0 / 5.0, -1.0 / 5.0, 4.0 / 105.0, -1.0 / 280.0)


def padded_2(cells, sides, width):
    for axis, dim in sides:
        count = lax.axis_size(axis)
        ends = count - 1
        head = lax.slice_in_dim(cells, 0, width, axis=dim)
        tail = lax.slice_in_dim(cells, cells.shape[dim] - width, cells.shape[dim], axis=dim)
        cells = jnp.concatenate(
            [
                lax.ppermute(tail, axis, [(i, (i + 1) % count) for i in range(ends)]),
                cells,
                lax.ppermute(head, axis, [((i + 1) % count, i) for i in range(ends)]),
            ],
            axis=dim,
        )
    return cells


def derivatives(padded, sx, sy, sz):

    def part(dx, dy, dz):
        return padded[:, 4 + dx : 4 + dx + sx, 4 + dy : 4 + dy + sy, 4 + dz : 4 + dz + sz]

    centre = part(0, 0, 0)
    dxx = second_coef[0] * centre
    dyy = second_coef[0] * centre
    dzz = second_coef[0] * centre
    for k in range(1, 5):
        dxx = dxx + second_coef[k] * (part(k, 0, 0) + part(-k, 0, 0))
        dyy = dyy + second_coef[k] * (part(0, k, 0) + part(0, -k, 0))
        dzz = dzz + second_coef[k] * (part(0, 0, k) + part(0, 0, -k))
    dy_wide = 0.0
    dz_xwide = 0.0
    dz_ywide = 0.0
    for k in range(1, 5):
        weight = first_coef[k - 1]
        dy_wide = dy_wide + weight * (
            padded[:, :, 4 + k : 4 + k + sy, 4 : 4 + sz]
            - padded[:, :, 4 - k : 4 - k + sy, 4 : 4 + sz]
        )
        dz_xwide = dz_xwide + weight * (
            padded[:, :, 4 : 4 + sy, 4 + k : 4 + k + sz]
            - padded[:, :, 4 : 4 + sy, 4 - k : 4 - k + sz]
        )
        dz_ywide = dz_ywide + weight * (
            padded[:, 4 : 4 + sx, :, 4 + k : 4 + k + sz]
            - padded[:, 4 : 4 + sx, :, 4 - k : 4 - k + sz]
        )
    dxy = 0.0
    dxz = 0.0
    dyz = 0.0
    for k in range(1, 5):
        weight = first_coef[k - 1]
        dxy = dxy + weight * (dy_wide[:, 4 + k : 4 + k + sx] - dy_wide[:, 4 - k : 4 - k + sx])
        dxz = dxz + weight * (dz_xwide[:, 4 + k : 4 + k + sx] - dz_xwide[:, 4 - k : 4 - k + sx])
        dyz = dyz + weight * (
            dz_ywide[:, :, 4 + k : 4 + k + sy] - dz_ywide[:, :, 4 - k : 4 - k + sy]
        )
    return (centre, dxx, dyy, dzz, dxy, dxz, dyz)


def advance(padded, previous, speed, epsilon, delta, theta, phi, source):
    sx, sy, sz = (previous.shape[1], previous.shape[2], previous.shape[3])
    centre, dxx, dyy, dzz, dxy, dxz, dyz = derivatives(padded, sx, sy, sz)
    axis_x = jnp.sin(theta) * jnp.cos(phi)
    axis_y = jnp.sin(theta) * jnp.sin(phi)
    axis_z = jnp.cos(theta)
    rotated = (
        axis_x * axis_x * dxx
        + axis_y * axis_y * dyy
        + axis_z * axis_z * dzz
        + 2.0 * axis_x * axis_y * dxy
        + 2.0 * axis_x * axis_z * dxz
        + 2.0 * axis_y * axis_z * dyz
    )
    remainder = dxx + dyy + dzz - rotated
    root_delta = jnp.sqrt(1.0 + 2.0 * delta)
    p_new = (
        2.0 * centre[0]
        - previous[0]
        + speed * ((1.0 + 2.0 * epsilon) * remainder[0] + root_delta * rotated[1])
        + source
    )
    q_new = (
        2.0 * centre[1] - previous[1] + speed * (root_delta * remainder[0] + rotated[1]) + source
    )
    return jnp.stack([p_new, q_new])


def pad_depth(fields):
    return jnp.pad(fields, ((0, 0), (0, 0), (0, 0), (4, 4)))


def from_neighbours(low_part, high_part, axis):
    count = lax.axis_size(axis)
    below = lax.ppermute(low_part, axis, [(i, i + 1) for i in range(count - 1)])
    above = lax.ppermute(high_part, axis, [(i + 1, i) for i in range(count - 1)])
    return below, above


def gather_column(traces, time_steps, rec_owner, rec_local):
    groups = lax.axis_size("gx")
    held = rec_local.shape[0]
    steps = jnp.arange(traces.shape[0], dtype=jnp.int32)
    chosen = (time_steps[:, None] == steps[None, :]).astype(jnp.float32)
    samples = jnp.dot(
        chosen, traces, precision=lax.Precision.HIGHEST, preferred_element_type=jnp.float32
    )
    payload = jnp.concatenate(
        [samples, rec_local.astype(jnp.float32)[None], rec_owner[:, 0].astype(jnp.float32)[None]]
    )
    if groups & (groups - 1) == 0:
        arrived = payload
        step = 1
        while step < groups:
            partner = lax.ppermute(arrived, "gx", [(i, i ^ step) for i in range(groups)])
            arrived = jnp.concatenate([arrived, partner], axis=1)
            step *= 2
        return arrived
    sent = jnp.broadcast_to(payload[None], (groups, 4, held))
    arrived = lax.all_to_all(sent, "gx", split_axis=0, concat_axis=0, tiled=True)
    return jnp.transpose(arrived, (1, 0, 2)).reshape(4, groups * held)


def sources_over(arrived, values, shape, first, rows):
    sx, sy, sz = shape
    cell = arrived[2].astype(jnp.int32)
    owner = arrived[3].astype(jnp.int32)
    row = (owner - lax.axis_index("gx")) * sx + cell // (sy * sz) - first
    inside = (row >= 0) & (row < rows)
    plane = jnp.where(inside, row * sy + cell // sz % sy, -1)
    depth = cell % sz
    picks = (plane[None, :] == jnp.arange(rows * sy, dtype=jnp.int32)[:, None]).astype(jnp.float32)
    spread = values[:, None, :] * picks[None, :, :]
    columns = (depth[:, None] == jnp.arange(sz, dtype=jnp.int32)[None, :]).astype(jnp.float32)
    sources = jnp.einsum(
        "cpr,rz->cpz", spread, columns, precision=lax.Precision.HIGHEST,
        preferred_element_type=jnp.float32,
    )
    return sources.reshape(values.shape[0], rows, sy, sz)


def local(
    p_now,
    q_now,
    p_prev,
    q_prev,
    speed,
    epsilon,
    delta,
    theta,
    phi,
    snapshots,
    traces,
    time_steps,
    rec_owner,
    rec_local,
):
    sx, sy, sz = p_now.shape
    assert sx == 8
    current = jnp.stack([p_now, q_now])
    earlier = jnp.stack([p_prev, q_prev])
    params = (speed, epsilon, delta, theta, phi)

    def slabs(parts):
        return jnp.concatenate([part.reshape(-1, sy, sz) for part in parts], axis=0)

    now_lo, now_hi = from_neighbours(
        slabs([p_now, q_now]).reshape(2, 8, sy, sz), slabs([p_now, q_now]).reshape(2, 8, sy, sz),
        "gx",
    )
    rest_lo, rest_hi = from_neighbours(
        slabs([p_prev[sx - 4 :], q_prev[sx - 4 :]] + [f[sx - 4 :] for f in params]),
        slabs([p_prev[:4], q_prev[:4]] + [f[:4] for f in params]),
        "gx",
    )

    def unpack(got):
        return got[0:8].reshape(2, 4, sy, sz), got[8:28].reshape(5, 4, sy, sz)

    (prev_lo, params_lo), (prev_hi, params_hi) = unpack(rest_lo), unpack(rest_hi)
    now_x = jnp.concatenate([now_lo, current, now_hi], axis=1)
    prev_x = jnp.concatenate([prev_lo, earlier, prev_hi], axis=1)
    params_x = [
        jnp.concatenate([params_lo[k], params[k], params_hi[k]], axis=0) for k in range(5)
    ]
    lo_y, hi_y = from_neighbours(now_x[:, :, sy - 4 :], now_x[:, :, :4], "gy")
    now_xy = pad_depth(jnp.concatenate([lo_y, now_x, hi_y], axis=2))

    arrived = gather_column(traces, time_steps, rec_owner, rec_local)
    source_0 = sources_over(arrived, arrived[0:1], (sx, sy, sz), -4, sx + 8)[0]
    source_1 = sources_over(arrived, arrived[1:2], (sx, sy, sz), 0, sx)[0]

    mid_x = advance(now_xy, prev_x, *params_x, source_0)
    middle = mid_x[:, 4 : 4 + sx]
    lo_m, hi_m = from_neighbours(mid_x[:, :, sy - 4 :], mid_x[:, :, :4], "gy")
    mid_xy = pad_depth(jnp.concatenate([lo_m, mid_x, hi_m], axis=2))
    final = advance(mid_xy, current, speed, epsilon, delta, theta, phi, source_1)
    image = (
        snapshots[0].astype(jnp.float32) * middle[0] + snapshots[1].astype(jnp.float32) * final[0]
    )
    return (final[0], final[1], middle[0], middle[1], image)


def solution(mesh):
    return jax.shard_map(
        local,
        mesh=mesh,
        in_specs=(
            P(("shots", "gx"), "gy", None),
            P(("shots", "gx"), "gy", None),
            P(("shots", "gx"), "gy", None),
            P(("shots", "gx"), "gy", None),
            P("gx", "gy", None),
            P("gx", "gy", None),
            P("gx", "gy", None),
            P("gx", "gy", None),
            P("gx", "gy", None),
            P(None, ("shots", "gx"), "gy", None),
            P(None, ("shots", "gx", "gy")),
            P("shots"),
            P(("shots", "gx", "gy"), None),
            P(("shots", "gx", "gy")),
        ),
        out_specs=(
            P(("shots", "gx"), "gy", None),
            P(("shots", "gx"), "gy", None),
            P(("shots", "gx"), "gy", None),
            P(("shots", "gx"), "gy", None),
            P(("shots", "gx"), "gy", None),
        ),
        check_vma=False,
    )
```

```python
import jax
import jax.numpy as jnp
from jax import lax
from jax.sharding import PartitionSpec as P

second_coef = (-205.0 / 72.0, 8.0 / 5.0, -1.0 / 5.0, 8.0 / 315.0, -1.0 / 560.0)
first_coef = (4.0 / 5.0, -1.0 / 5.0, 4.0 / 105.0, -1.0 / 280.0)


def padded_2(cells, sides, width):
    for axis, dim in sides:
        count = lax.axis_size(axis)
        ends = count - 1
        head = lax.slice_in_dim(cells, 0, width, axis=dim)
        tail = lax.slice_in_dim(cells, cells.shape[dim] - width, cells.shape[dim], axis=dim)
        cells = jnp.concatenate(
            [
                lax.ppermute(tail, axis, [(i, (i + 1) % count) for i in range(ends)]),
                cells,
                lax.ppermute(head, axis, [((i + 1) % count, i) for i in range(ends)]),
            ],
            axis=dim,
        )
    return cells


def derivatives(padded, sx, sy, sz):

    def part(dx, dy, dz):
        return padded[:, 4 + dx : 4 + dx + sx, 4 + dy : 4 + dy + sy, 4 + dz : 4 + dz + sz]

    centre = part(0, 0, 0)
    dxx = second_coef[0] * centre
    dyy = second_coef[0] * centre
    dzz = second_coef[0] * centre
    for k in range(1, 5):
        dxx = dxx + second_coef[k] * (part(k, 0, 0) + part(-k, 0, 0))
        dyy = dyy + second_coef[k] * (part(0, k, 0) + part(0, -k, 0))
        dzz = dzz + second_coef[k] * (part(0, 0, k) + part(0, 0, -k))
    dy_wide = 0.0
    dz_xwide = 0.0
    dz_ywide = 0.0
    for k in range(1, 5):
        weight = first_coef[k - 1]
        dy_wide = dy_wide + weight * (
            padded[:, :, 4 + k : 4 + k + sy, 4 : 4 + sz]
            - padded[:, :, 4 - k : 4 - k + sy, 4 : 4 + sz]
        )
        dz_xwide = dz_xwide + weight * (
            padded[:, :, 4 : 4 + sy, 4 + k : 4 + k + sz]
            - padded[:, :, 4 : 4 + sy, 4 - k : 4 - k + sz]
        )
        dz_ywide = dz_ywide + weight * (
            padded[:, 4 : 4 + sx, :, 4 + k : 4 + k + sz]
            - padded[:, 4 : 4 + sx, :, 4 - k : 4 - k + sz]
        )
    dxy = 0.0
    dxz = 0.0
    dyz = 0.0
    for k in range(1, 5):
        weight = first_coef[k - 1]
        dxy = dxy + weight * (dy_wide[:, 4 + k : 4 + k + sx] - dy_wide[:, 4 - k : 4 - k + sx])
        dxz = dxz + weight * (dz_xwide[:, 4 + k : 4 + k + sx] - dz_xwide[:, 4 - k : 4 - k + sx])
        dyz = dyz + weight * (
            dz_ywide[:, :, 4 + k : 4 + k + sy] - dz_ywide[:, :, 4 - k : 4 - k + sy]
        )
    return (centre, dxx, dyy, dzz, dxy, dxz, dyz)


def coefficients(epsilon, delta, theta, phi):
    axis_x = jnp.sin(theta) * jnp.cos(phi)
    axis_y = jnp.sin(theta) * jnp.sin(phi)
    axis_z = jnp.cos(theta)
    return (
        axis_x * axis_x,
        axis_y * axis_y,
        axis_z * axis_z,
        2.0 * axis_x * axis_y,
        2.0 * axis_x * axis_z,
        2.0 * axis_y * axis_z,
        1.0 + 2.0 * epsilon,
        jnp.sqrt(1.0 + 2.0 * delta),
    )


def advance(padded, previous, speed, coefs, source):
    sx, sy, sz = (previous.shape[1], previous.shape[2], previous.shape[3])
    centre, dxx, dyy, dzz, dxy, dxz, dyz = derivatives(padded, sx, sy, sz)
    nxx, nyy, nzz, nxy, nxz, nyz, stretch, root_delta = coefs
    rotated = nxx * dxx + nyy * dyy + nzz * dzz + nxy * dxy + nxz * dxz + nyz * dyz
    remainder = dxx + dyy + dzz - rotated
    p_new = (
        2.0 * centre[0]
        - previous[0]
        + speed * (stretch * remainder[0] + root_delta * rotated[1])
        + source
    )
    q_new = (
        2.0 * centre[1] - previous[1] + speed * (root_delta * remainder[0] + rotated[1]) + source
    )
    return jnp.stack([p_new, q_new])


def pad_depth(fields):
    return jnp.pad(fields, ((0, 0), (0, 0), (0, 0), (4, 4)))


def from_neighbours(low_part, high_part, axis):
    count = lax.axis_size(axis)
    below = lax.ppermute(low_part, axis, [(i, i + 1) for i in range(count - 1)])
    above = lax.ppermute(high_part, axis, [(i + 1, i) for i in range(count - 1)])
    return below, above


def gather_column(traces, time_steps, rec_owner, rec_local):
    groups = lax.axis_size("gx")
    held = rec_local.shape[0]
    steps = jnp.arange(traces.shape[0], dtype=jnp.int32)
    chosen = (time_steps[:, None] == steps[None, :]).astype(jnp.float32)
    samples = jnp.dot(
        chosen, traces, precision=lax.Precision.HIGHEST, preferred_element_type=jnp.float32
    )
    payload = jnp.concatenate(
        [samples, rec_local.astype(jnp.float32)[None], rec_owner[:, 0].astype(jnp.float32)[None]]
    )
    if groups & (groups - 1) == 0:
        arrived = payload
        step = 1
        while step < groups:
            partner = lax.ppermute(arrived, "gx", [(i, i ^ step) for i in range(groups)])
            arrived = jnp.concatenate([arrived, partner], axis=1)
            step *= 2
        return arrived
    sent = jnp.broadcast_to(payload[None], (groups, 4, held))
    arrived = lax.all_to_all(sent, "gx", split_axis=0, concat_axis=0, tiled=True)
    return jnp.transpose(arrived, (1, 0, 2)).reshape(4, groups * held)


def sources_over(arrived, values, shape, first, rows):
    sx, sy, sz = shape
    cell = arrived[2].astype(jnp.int32)
    owner = arrived[3].astype(jnp.int32)
    row = (owner - lax.axis_index("gx")) * sx + cell // (sy * sz) - first
    inside = (row >= 0) & (row < rows)
    plane = jnp.where(inside, row * sy + cell // sz % sy, -1)
    depth = cell % sz
    picks = (plane[None, :] == jnp.arange(rows * sy, dtype=jnp.int32)[:, None]).astype(jnp.float32)
    spread = values[:, None, :] * picks[None, :, :]
    columns = (depth[:, None] == jnp.arange(sz, dtype=jnp.int32)[None, :]).astype(jnp.float32)
    sources = jnp.einsum(
        "cpr,rz->cpz", spread, columns, precision=lax.Precision.HIGHEST,
        preferred_element_type=jnp.float32,
    )
    return sources.reshape(values.shape[0], rows, sy, sz)


def local(
    p_now,
    q_now,
    p_prev,
    q_prev,
    speed,
    epsilon,
    delta,
    theta,
    phi,
    snapshots,
    traces,
    time_steps,
    rec_owner,
    rec_local,
):
    sx, sy, sz = p_now.shape
    assert sx == 8
    current = jnp.stack([p_now, q_now])
    earlier = jnp.stack([p_prev, q_prev])
    params = (speed, epsilon, delta, theta, phi)

    def slabs(parts):
        return jnp.concatenate([part.reshape(-1, sy, sz) for part in parts], axis=0)

    low_part = slabs(
        [p_now, q_now, p_prev[sx - 4 :], q_prev[sx - 4 :]] + [f[sx - 4 :] for f in params]
    )
    high_part = slabs([p_now, q_now, p_prev[:4], q_prev[:4]] + [f[:4] for f in params])
    below, above = from_neighbours(low_part, high_part, "gx")

    def unpack(got):
        return (
            got[0:16].reshape(2, 8, sy, sz),
            got[16:24].reshape(2, 4, sy, sz),
            got[24:44].reshape(5, 4, sy, sz),
        )

    (now_lo, prev_lo, params_lo), (now_hi, prev_hi, params_hi) = unpack(below), unpack(above)
    now_x = jnp.concatenate([now_lo, current, now_hi], axis=1)
    prev_x = jnp.concatenate([prev_lo, earlier, prev_hi], axis=1)
    coefs = coefficients(epsilon, delta, theta, phi)
    coefs_lo = coefficients(*params_lo[1:5])
    coefs_hi = coefficients(*params_hi[1:5])
    coefs_x = [jnp.concatenate(parts, axis=0) for parts in zip(coefs_lo, coefs, coefs_hi)]
    speed_x = jnp.concatenate([params_lo[0], speed, params_hi[0]], axis=0)
    lo_y, hi_y = from_neighbours(now_x[:, :, sy - 4 :], now_x[:, :, :4], "gy")
    now_xy = pad_depth(jnp.concatenate([lo_y, now_x, hi_y], axis=2))

    arrived = gather_column(traces, time_steps, rec_owner, rec_local)
    source_0 = sources_over(arrived, arrived[0:1], (sx, sy, sz), -4, sx + 8)[0]
    source_1 = sources_over(arrived, arrived[1:2], (sx, sy, sz), 0, sx)[0]

    mid_x = advance(now_xy, prev_x, speed_x, coefs_x, source_0)
    middle = mid_x[:, 4 : 4 + sx]
    lo_m, hi_m = from_neighbours(mid_x[:, :, sy - 4 :], mid_x[:, :, :4], "gy")
    mid_xy = pad_depth(jnp.concatenate([lo_m, mid_x, hi_m], axis=2))
    final = advance(mid_xy, current, speed, coefs, source_1)
    image = (
        snapshots[0].astype(jnp.float32) * middle[0] + snapshots[1].astype(jnp.float32) * final[0]
    )
    return (final[0], final[1], middle[0], middle[1], image)


def solution(mesh):
    return jax.shard_map(
        local,
        mesh=mesh,
        in_specs=(
            P(("shots", "gx"), "gy", None),
            P(("shots", "gx"), "gy", None),
            P(("shots", "gx"), "gy", None),
            P(("shots", "gx"), "gy", None),
            P("gx", "gy", None),
            P("gx", "gy", None),
            P("gx", "gy", None),
            P("gx", "gy", None),
            P("gx", "gy", None),
            P(None, ("shots", "gx"), "gy", None),
            P(None, ("shots", "gx", "gy")),
            P("shots"),
            P(("shots", "gx", "gy"), None),
            P(("shots", "gx", "gy")),
        ),
        out_specs=(
            P(("shots", "gx"), "gy", None),
            P(("shots", "gx"), "gy", None),
            P(("shots", "gx"), "gy", None),
            P(("shots", "gx"), "gy", None),
            P(("shots", "gx"), "gy", None),
        ),
        check_vma=False,
    )
```

```python
import jax
import jax.numpy as jnp
from jax import lax
from jax.sharding import PartitionSpec as P

second_coef = (-205.0 / 72.0, 8.0 / 5.0, -1.0 / 5.0, 8.0 / 315.0, -1.0 / 560.0)
first_coef = (4.0 / 5.0, -1.0 / 5.0, 4.0 / 105.0, -1.0 / 280.0)


def padded_2(cells, sides, width):
    for axis, dim in sides:
        count = lax.axis_size(axis)
        ends = count - 1
        head = lax.slice_in_dim(cells, 0, width, axis=dim)
        tail = lax.slice_in_dim(cells, cells.shape[dim] - width, cells.shape[dim], axis=dim)
        cells = jnp.concatenate(
            [
                lax.ppermute(tail, axis, [(i, (i + 1) % count) for i in range(ends)]),
                cells,
                lax.ppermute(head, axis, [((i + 1) % count, i) for i in range(ends)]),
            ],
            axis=dim,
        )
    return cells


def derivatives(padded, sx, sy, sz):

    def part(dx, dy, dz):
        return padded[:, 4 + dx : 4 + dx + sx, 4 + dy : 4 + dy + sy, 4 + dz : 4 + dz + sz]

    centre = part(0, 0, 0)
    dxx = second_coef[0] * centre
    dyy = second_coef[0] * centre
    dzz = second_coef[0] * centre
    for k in range(1, 5):
        dxx = dxx + second_coef[k] * (part(k, 0, 0) + part(-k, 0, 0))
        dyy = dyy + second_coef[k] * (part(0, k, 0) + part(0, -k, 0))
        dzz = dzz + second_coef[k] * (part(0, 0, k) + part(0, 0, -k))
    dy_wide = 0.0
    dz_xwide = 0.0
    dz_ywide = 0.0
    for k in range(1, 5):
        weight = first_coef[k - 1]
        dy_wide = dy_wide + weight * (
            padded[:, :, 4 + k : 4 + k + sy, 4 : 4 + sz]
            - padded[:, :, 4 - k : 4 - k + sy, 4 : 4 + sz]
        )
        dz_xwide = dz_xwide + weight * (
            padded[:, :, 4 : 4 + sy, 4 + k : 4 + k + sz]
            - padded[:, :, 4 : 4 + sy, 4 - k : 4 - k + sz]
        )
        dz_ywide = dz_ywide + weight * (
            padded[:, 4 : 4 + sx, :, 4 + k : 4 + k + sz]
            - padded[:, 4 : 4 + sx, :, 4 - k : 4 - k + sz]
        )
    dxy = 0.0
    dxz = 0.0
    dyz = 0.0
    for k in range(1, 5):
        weight = first_coef[k - 1]
        dxy = dxy + weight * (dy_wide[:, 4 + k : 4 + k + sx] - dy_wide[:, 4 - k : 4 - k + sx])
        dxz = dxz + weight * (dz_xwide[:, 4 + k : 4 + k + sx] - dz_xwide[:, 4 - k : 4 - k + sx])
        dyz = dyz + weight * (
            dz_ywide[:, :, 4 + k : 4 + k + sy] - dz_ywide[:, :, 4 - k : 4 - k + sy]
        )
    return (centre, dxx, dyy, dzz, dxy, dxz, dyz)


def coefficients(epsilon, delta, theta, phi):
    axis_x = jnp.sin(theta) * jnp.cos(phi)
    axis_y = jnp.sin(theta) * jnp.sin(phi)
    axis_z = jnp.cos(theta)
    return (
        axis_x * axis_x,
        axis_y * axis_y,
        axis_z * axis_z,
        2.0 * axis_x * axis_y,
        2.0 * axis_x * axis_z,
        2.0 * axis_y * axis_z,
        1.0 + 2.0 * epsilon,
        jnp.sqrt(1.0 + 2.0 * delta),
    )


def advance(padded, previous, speed, coefs, source):
    sx, sy, sz = (previous.shape[1], previous.shape[2], previous.shape[3])
    centre, dxx, dyy, dzz, dxy, dxz, dyz = derivatives(padded, sx, sy, sz)
    nxx, nyy, nzz, nxy, nxz, nyz, stretch, root_delta = coefs
    rotated = nxx * dxx + nyy * dyy + nzz * dzz + nxy * dxy + nxz * dxz + nyz * dyz
    remainder = dxx + dyy + dzz - rotated
    p_new = (
        2.0 * centre[0]
        - previous[0]
        + speed * (stretch * remainder[0] + root_delta * rotated[1])
        + source
    )
    q_new = (
        2.0 * centre[1] - previous[1] + speed * (root_delta * remainder[0] + rotated[1]) + source
    )
    return jnp.stack([p_new, q_new])


def pad_depth(fields):
    return jnp.pad(fields, ((0, 0), (0, 0), (0, 0), (4, 4)))


def from_neighbours(low_part, high_part, axis):
    count = lax.axis_size(axis)
    below = lax.ppermute(low_part, axis, [(i, i + 1) for i in range(count - 1)])
    above = lax.ppermute(high_part, axis, [(i + 1, i) for i in range(count - 1)])
    return below, above


def gather_column(traces, time_steps, rec_owner, rec_local):
    groups = lax.axis_size("gx")
    held = rec_local.shape[0]
    steps = jnp.arange(traces.shape[0], dtype=jnp.int32)
    chosen = (time_steps[:, None] == steps[None, :]).astype(jnp.float32)
    samples = jnp.dot(
        chosen, traces, precision=lax.Precision.HIGHEST, preferred_element_type=jnp.float32
    )
    payload = jnp.concatenate(
        [samples, rec_local.astype(jnp.float32)[None], rec_owner[:, 0].astype(jnp.float32)[None]]
    )
    if groups & (groups - 1) == 0:
        arrived = payload
        step = 1
        while step < groups:
            partner = lax.ppermute(arrived, "gx", [(i, i ^ step) for i in range(groups)])
            arrived = jnp.concatenate([arrived, partner], axis=1)
            step *= 2
        return arrived
    sent = jnp.broadcast_to(payload[None], (groups, 4, held))
    arrived = lax.all_to_all(sent, "gx", split_axis=0, concat_axis=0, tiled=True)
    return jnp.transpose(arrived, (1, 0, 2)).reshape(4, groups * held)


def sources_over(arrived, values, shape, first, rows):
    sx, sy, sz = shape
    cell = arrived[2].astype(jnp.int32)
    owner = arrived[3].astype(jnp.int32)
    row = (owner - lax.axis_index("gx")) * sx + cell // (sy * sz) - first
    inside = (row >= 0) & (row < rows)
    plane = jnp.where(inside, row * sy + cell // sz % sy, -1)
    depth = cell % sz
    picks = (plane[None, :] == jnp.arange(rows * sy, dtype=jnp.int32)[:, None]).astype(jnp.float32)
    spread = values[:, None, :] * picks[None, :, :]
    columns = (depth[:, None] == jnp.arange(sz, dtype=jnp.int32)[None, :]).astype(jnp.float32)
    sources = jnp.einsum(
        "cpr,rz->cpz", spread, columns, precision=lax.Precision.HIGHEST,
        preferred_element_type=jnp.float32,
    )
    return sources.reshape(values.shape[0], rows, sy, sz)


def local(
    p_now,
    q_now,
    p_prev,
    q_prev,
    speed,
    epsilon,
    delta,
    theta,
    phi,
    snapshots,
    traces,
    time_steps,
    rec_owner,
    rec_local,
):
    sx, sy, sz = p_now.shape
    assert sx == 8
    current = jnp.stack([p_now, q_now])
    earlier = jnp.stack([p_prev, q_prev])
    params = (speed, epsilon, delta, theta, phi)

    def slabs(parts):
        return jnp.concatenate([part.reshape(-1, sy, sz) for part in parts], axis=0)

    low_part = slabs(
        [p_now, q_now, p_prev[sx - 4 :], q_prev[sx - 4 :]] + [f[sx - 4 :] for f in params]
    )
    high_part = slabs([p_now, q_now, p_prev[:4], q_prev[:4]] + [f[:4] for f in params])
    below, above = from_neighbours(low_part, high_part, "gx")

    def unpack(got):
        return (
            got[0:16].reshape(2, 8, sy, sz),
            got[16:24].reshape(2, 4, sy, sz),
            got[24:44].reshape(5, 4, sy, sz),
        )

    (now_lo, prev_lo, params_lo), (now_hi, prev_hi, params_hi) = unpack(below), unpack(above)
    now_x = jnp.concatenate([now_lo, current, now_hi], axis=1)
    prev_x = jnp.concatenate([prev_lo, earlier, prev_hi], axis=1)
    coefs = coefficients(epsilon, delta, theta, phi)
    coefs_lo = coefficients(*params_lo[1:5])
    coefs_hi = coefficients(*params_hi[1:5])
    coefs_x = [jnp.concatenate(parts, axis=0) for parts in zip(coefs_lo, coefs, coefs_hi)]
    speed_x = jnp.concatenate([params_lo[0], speed, params_hi[0]], axis=0)
    lo_y, hi_y = from_neighbours(now_x[:, :, sy - 4 :], now_x[:, :, :4], "gy")
    now_xy = pad_depth(jnp.concatenate([lo_y, now_x, hi_y], axis=2))

    arrived = gather_column(traces, time_steps, rec_owner, rec_local)
    arrived = arrived + 0.0 * (lo_y[0, 0, 0, 0] + hi_y[0, 0, 0, 0])
    source_0 = sources_over(arrived, arrived[0:1], (sx, sy, sz), -4, sx + 8)[0]
    source_1 = sources_over(arrived, arrived[1:2], (sx, sy, sz), 0, sx)[0]

    mid_x = advance(now_xy, prev_x, speed_x, coefs_x, source_0)
    middle = mid_x[:, 4 : 4 + sx]
    lo_m, hi_m = from_neighbours(mid_x[:, :, sy - 4 :], mid_x[:, :, :4], "gy")
    mid_xy = pad_depth(jnp.concatenate([lo_m, mid_x, hi_m], axis=2))
    final = advance(mid_xy, current, speed, coefs, source_1)
    image = (
        snapshots[0].astype(jnp.float32) * middle[0] + snapshots[1].astype(jnp.float32) * final[0]
    )
    return (final[0], final[1], middle[0], middle[1], image)


def solution(mesh):
    return jax.shard_map(
        local,
        mesh=mesh,
        in_specs=(
            P(("shots", "gx"), "gy", None),
            P(("shots", "gx"), "gy", None),
            P(("shots", "gx"), "gy", None),
            P(("shots", "gx"), "gy", None),
            P("gx", "gy", None),
            P("gx", "gy", None),
            P("gx", "gy", None),
            P("gx", "gy", None),
            P("gx", "gy", None),
            P(None, ("shots", "gx"), "gy", None),
            P(None, ("shots", "gx", "gy")),
            P("shots"),
            P(("shots", "gx", "gy"), None),
            P(("shots", "gx", "gy")),
        ),
        out_specs=(
            P(("shots", "gx"), "gy", None),
            P(("shots", "gx"), "gy", None),
            P(("shots", "gx"), "gy", None),
            P(("shots", "gx"), "gy", None),
            P(("shots", "gx"), "gy", None),
        ),
        check_vma=False,
    )
```

```python
import jax
import jax.numpy as jnp
from jax import lax
from jax.experimental import pallas as pl
from jax.experimental.pallas import tpu as pltpu
from jax.sharding import PartitionSpec as P

second_coef = (-205.0 / 72.0, 8.0 / 5.0, -1.0 / 5.0, 8.0 / 315.0, -1.0 / 560.0)
first_coef = (4.0 / 5.0, -1.0 / 5.0, 4.0 / 105.0, -1.0 / 280.0)


def padded_2(cells, sides, width):
    for axis, dim in sides:
        count = lax.axis_size(axis)
        ends = count - 1
        head = lax.slice_in_dim(cells, 0, width, axis=dim)
        tail = lax.slice_in_dim(cells, cells.shape[dim] - width, cells.shape[dim], axis=dim)
        cells = jnp.concatenate(
            [
                lax.ppermute(tail, axis, [(i, (i + 1) % count) for i in range(ends)]),
                cells,
                lax.ppermute(head, axis, [((i + 1) % count, i) for i in range(ends)]),
            ],
            axis=dim,
        )
    return cells


def derivatives(padded, sx, sy, sz):

    def part(dx, dy, dz):
        return padded[:, 4 + dx : 4 + dx + sx, 4 + dy : 4 + dy + sy, 4 + dz : 4 + dz + sz]

    centre = part(0, 0, 0)
    dxx = second_coef[0] * centre
    dyy = second_coef[0] * centre
    dzz = second_coef[0] * centre
    for k in range(1, 5):
        dxx = dxx + second_coef[k] * (part(k, 0, 0) + part(-k, 0, 0))
        dyy = dyy + second_coef[k] * (part(0, k, 0) + part(0, -k, 0))
        dzz = dzz + second_coef[k] * (part(0, 0, k) + part(0, 0, -k))
    dy_wide = 0.0
    dz_xwide = 0.0
    dz_ywide = 0.0
    for k in range(1, 5):
        weight = first_coef[k - 1]
        dy_wide = dy_wide + weight * (
            padded[:, :, 4 + k : 4 + k + sy, 4 : 4 + sz]
            - padded[:, :, 4 - k : 4 - k + sy, 4 : 4 + sz]
        )
        dz_xwide = dz_xwide + weight * (
            padded[:, :, 4 : 4 + sy, 4 + k : 4 + k + sz]
            - padded[:, :, 4 : 4 + sy, 4 - k : 4 - k + sz]
        )
        dz_ywide = dz_ywide + weight * (
            padded[:, 4 : 4 + sx, :, 4 + k : 4 + k + sz]
            - padded[:, 4 : 4 + sx, :, 4 - k : 4 - k + sz]
        )
    dxy = 0.0
    dxz = 0.0
    dyz = 0.0
    for k in range(1, 5):
        weight = first_coef[k - 1]
        dxy = dxy + weight * (dy_wide[:, 4 + k : 4 + k + sx] - dy_wide[:, 4 - k : 4 - k + sx])
        dxz = dxz + weight * (dz_xwide[:, 4 + k : 4 + k + sx] - dz_xwide[:, 4 - k : 4 - k + sx])
        dyz = dyz + weight * (
            dz_ywide[:, :, 4 + k : 4 + k + sy] - dz_ywide[:, :, 4 - k : 4 - k + sy]
        )
    return (centre, dxx, dyy, dzz, dxy, dxz, dyz)


def coefficients(epsilon, delta, theta, phi):
    axis_x = jnp.sin(theta) * jnp.cos(phi)
    axis_y = jnp.sin(theta) * jnp.sin(phi)
    axis_z = jnp.cos(theta)
    return (
        axis_x * axis_x,
        axis_y * axis_y,
        axis_z * axis_z,
        2.0 * axis_x * axis_y,
        2.0 * axis_x * axis_z,
        2.0 * axis_y * axis_z,
        1.0 + 2.0 * epsilon,
        jnp.sqrt(1.0 + 2.0 * delta),
    )


def advance(padded, previous, speed, coefs, source):
    sx, sy, sz = (previous.shape[1], previous.shape[2], previous.shape[3])
    centre, dxx, dyy, dzz, dxy, dxz, dyz = derivatives(padded, sx, sy, sz)
    nxx, nyy, nzz, nxy, nxz, nyz, stretch, root_delta = coefs
    rotated = nxx * dxx + nyy * dyy + nzz * dzz + nxy * dxy + nxz * dxz + nyz * dyz
    remainder = dxx + dyy + dzz - rotated
    p_new = (
        2.0 * centre[0]
        - previous[0]
        + speed * (stretch * remainder[0] + root_delta * rotated[1])
        + source
    )
    q_new = (
        2.0 * centre[1] - previous[1] + speed * (root_delta * remainder[0] + rotated[1]) + source
    )
    return jnp.stack([p_new, q_new])


def step_kernel(padded_ref, previous_ref, speed_ref, *rest):
    coef_refs, source_ref, out_ref = rest[:8], rest[8], rest[9]
    _, sx, sy, sz = out_ref.shape
    ny = padded_ref.shape[2]
    padded = padded_ref[...]

    def along_y(values, shift):
        return pltpu.roll(values, (-shift) % ny, 2)[:, :, 8 : 8 + sy]

    def along_z(values, shift):
        lane = lax.broadcasted_iota(jnp.int32, values.shape, 3)
        moved = pltpu.roll(values, (-shift) % sz, 3)
        return jnp.where((lane + shift >= 0) & (lane + shift < sz), moved, 0.0)

    own_x = padded[:, 4 : 4 + sx]
    own_y = padded[:, :, 8 : 8 + sy]
    centre = own_x[:, :, 8 : 8 + sy]
    dxx = second_coef[0] * centre
    dyy = second_coef[0] * centre
    dzz = second_coef[0] * centre
    for k in range(1, 5):
        dxx = dxx + second_coef[k] * (own_y[:, 4 + k : 4 + k + sx] + own_y[:, 4 - k : 4 - k + sx])
        dyy = dyy + second_coef[k] * (along_y(own_x, k) + along_y(own_x, -k))
        dzz = dzz + second_coef[k] * (along_z(centre, k) + along_z(centre, -k))
    dy_wide = 0.0
    dz_xwide = 0.0
    dz_ywide = 0.0
    for k in range(1, 5):
        weight = first_coef[k - 1]
        dy_wide = dy_wide + weight * (along_y(padded, k) - along_y(padded, -k))
        dz_xwide = dz_xwide + weight * (along_z(own_y, k) - along_z(own_y, -k))
        dz_ywide = dz_ywide + weight * (along_z(own_x, k) - along_z(own_x, -k))
    dxy = 0.0
    dxz = 0.0
    dyz = 0.0
    for k in range(1, 5):
        weight = first_coef[k - 1]
        dxy = dxy + weight * (dy_wide[:, 4 + k : 4 + k + sx] - dy_wide[:, 4 - k : 4 - k + sx])
        dxz = dxz + weight * (dz_xwide[:, 4 + k : 4 + k + sx] - dz_xwide[:, 4 - k : 4 - k + sx])
        dyz = dyz + weight * (along_y(dz_ywide, k) - along_y(dz_ywide, -k))
    nxx, nyy, nzz, nxy, nxz, nyz, stretch, root_delta = [ref[...] for ref in coef_refs]
    rotated = nxx * dxx + nyy * dyy + nzz * dzz + nxy * dxy + nxz * dxz + nyz * dyz
    remainder = dxx + dyy + dzz - rotated
    speed = speed_ref[...]
    source = source_ref[...]
    out_ref[0] = (
        2.0 * centre[0]
        - previous_ref[0]
        + speed * (stretch * remainder[0] + root_delta * rotated[1])
        + source
    )
    out_ref[1] = (
        2.0 * centre[1] - previous_ref[1] + speed * (root_delta * remainder[0] + rotated[1]) + source
    )


def advance_kernel(widened_xy, previous, speed, coefs, source):
    padded = jnp.pad(widened_xy, ((0, 0), (0, 0), (4, 4), (0, 0)))
    vmem = pl.BlockSpec(memory_space=pltpu.VMEM)
    return pl.pallas_call(
        step_kernel,
        out_shape=jax.ShapeDtypeStruct(previous.shape, jnp.float32),
        in_specs=[vmem] * 12,
        out_specs=vmem,
    )(padded, previous, speed, *coefs, source)


def pad_depth(fields):
    return jnp.pad(fields, ((0, 0), (0, 0), (0, 0), (4, 4)))


def from_neighbours(low_part, high_part, axis):
    count = lax.axis_size(axis)
    below = lax.ppermute(low_part, axis, [(i, i + 1) for i in range(count - 1)])
    above = lax.ppermute(high_part, axis, [(i + 1, i) for i in range(count - 1)])
    return below, above


def gather_column(traces, time_steps, rec_owner, rec_local):
    groups = lax.axis_size("gx")
    held = rec_local.shape[0]
    steps = jnp.arange(traces.shape[0], dtype=jnp.int32)
    chosen = (time_steps[:, None] == steps[None, :]).astype(jnp.float32)
    samples = jnp.dot(
        chosen, traces, precision=lax.Precision.HIGHEST, preferred_element_type=jnp.float32
    )
    payload = jnp.concatenate(
        [samples, rec_local.astype(jnp.float32)[None], rec_owner[:, 0].astype(jnp.float32)[None]]
    )
    if groups & (groups - 1) == 0:
        arrived = payload
        step = 1
        while step < groups:
            partner = lax.ppermute(arrived, "gx", [(i, i ^ step) for i in range(groups)])
            arrived = jnp.concatenate([arrived, partner], axis=1)
            step *= 2
        return arrived
    sent = jnp.broadcast_to(payload[None], (groups, 4, held))
    arrived = lax.all_to_all(sent, "gx", split_axis=0, concat_axis=0, tiled=True)
    return jnp.transpose(arrived, (1, 0, 2)).reshape(4, groups * held)


def sources_over(arrived, values, shape, first, rows):
    sx, sy, sz = shape
    cell = arrived[2].astype(jnp.int32)
    owner = arrived[3].astype(jnp.int32)
    row = (owner - lax.axis_index("gx")) * sx + cell // (sy * sz) - first
    inside = (row >= 0) & (row < rows)
    plane = jnp.where(inside, row * sy + cell // sz % sy, -1)
    depth = cell % sz
    picks = (plane[None, :] == jnp.arange(rows * sy, dtype=jnp.int32)[:, None]).astype(jnp.float32)
    spread = values[:, None, :] * picks[None, :, :]
    columns = (depth[:, None] == jnp.arange(sz, dtype=jnp.int32)[None, :]).astype(jnp.float32)
    sources = jnp.einsum(
        "cpr,rz->cpz", spread, columns, precision=lax.Precision.HIGHEST,
        preferred_element_type=jnp.float32,
    )
    return sources.reshape(values.shape[0], rows, sy, sz)


def local(
    p_now,
    q_now,
    p_prev,
    q_prev,
    speed,
    epsilon,
    delta,
    theta,
    phi,
    snapshots,
    traces,
    time_steps,
    rec_owner,
    rec_local,
):
    sx, sy, sz = p_now.shape
    assert sx == 8
    current = jnp.stack([p_now, q_now])
    earlier = jnp.stack([p_prev, q_prev])
    params = (speed, epsilon, delta, theta, phi)

    def slabs(parts):
        return jnp.concatenate([part.reshape(-1, sy, sz) for part in parts], axis=0)

    low_part = slabs(
        [p_now, q_now, p_prev[sx - 4 :], q_prev[sx - 4 :]] + [f[sx - 4 :] for f in params]
    )
    high_part = slabs([p_now, q_now, p_prev[:4], q_prev[:4]] + [f[:4] for f in params])
    below, above = from_neighbours(low_part, high_part, "gx")

    def unpack(got):
        return (
            got[0:16].reshape(2, 8, sy, sz),
            got[16:24].reshape(2, 4, sy, sz),
            got[24:44].reshape(5, 4, sy, sz),
        )

    (now_lo, prev_lo, params_lo), (now_hi, prev_hi, params_hi) = unpack(below), unpack(above)
    now_x = jnp.concatenate([now_lo, current, now_hi], axis=1)
    prev_x = jnp.concatenate([prev_lo, earlier, prev_hi], axis=1)
    coefs = coefficients(epsilon, delta, theta, phi)
    coefs_lo = coefficients(*params_lo[1:5])
    coefs_hi = coefficients(*params_hi[1:5])
    coefs_x = [jnp.concatenate(parts, axis=0) for parts in zip(coefs_lo, coefs, coefs_hi)]
    speed_x = jnp.concatenate([params_lo[0], speed, params_hi[0]], axis=0)
    lo_y, hi_y = from_neighbours(now_x[:, :, sy - 4 :], now_x[:, :, :4], "gy")
    now_xy = jnp.concatenate([lo_y, now_x, hi_y], axis=2)

    arrived = gather_column(traces, time_steps, rec_owner, rec_local)
    source_0 = sources_over(arrived, arrived[0:1], (sx, sy, sz), -4, sx + 8)[0]
    source_1 = sources_over(arrived, arrived[1:2], (sx, sy, sz), 0, sx)[0]

    mid_x = advance_kernel(now_xy, prev_x, speed_x, coefs_x, source_0)
    middle = mid_x[:, 4 : 4 + sx]
    lo_m, hi_m = from_neighbours(mid_x[:, :, sy - 4 :], mid_x[:, :, :4], "gy")
    mid_xy = jnp.concatenate([lo_m, mid_x, hi_m], axis=2)
    final = advance_kernel(mid_xy, current, speed, coefs, source_1)
    image = (
        snapshots[0].astype(jnp.float32) * middle[0] + snapshots[1].astype(jnp.float32) * final[0]
    )
    return (final[0], final[1], middle[0], middle[1], image)


def solution(mesh):
    return jax.shard_map(
        local,
        mesh=mesh,
        in_specs=(
            P(("shots", "gx"), "gy", None),
            P(("shots", "gx"), "gy", None),
            P(("shots", "gx"), "gy", None),
            P(("shots", "gx"), "gy", None),
            P("gx", "gy", None),
            P("gx", "gy", None),
            P("gx", "gy", None),
            P("gx", "gy", None),
            P("gx", "gy", None),
            P(None, ("shots", "gx"), "gy", None),
            P(None, ("shots", "gx", "gy")),
            P("shots"),
            P(("shots", "gx", "gy"), None),
            P(("shots", "gx", "gy")),
        ),
        out_specs=(
            P(("shots", "gx"), "gy", None),
            P(("shots", "gx"), "gy", None),
            P(("shots", "gx"), "gy", None),
            P(("shots", "gx"), "gy", None),
            P(("shots", "gx"), "gy", None),
        ),
        check_vma=False,
    )
```

```python
import jax
import jax.numpy as jnp
from jax import lax
from jax.sharding import PartitionSpec as P

second_coef = (-205.0 / 72.0, 8.0 / 5.0, -1.0 / 5.0, 8.0 / 315.0, -1.0 / 560.0)
first_coef = (4.0 / 5.0, -1.0 / 5.0, 4.0 / 105.0, -1.0 / 280.0)


def padded_2(cells, sides, width):
    for axis, dim in sides:
        count = lax.axis_size(axis)
        ends = count - 1
        head = lax.slice_in_dim(cells, 0, width, axis=dim)
        tail = lax.slice_in_dim(cells, cells.shape[dim] - width, cells.shape[dim], axis=dim)
        cells = jnp.concatenate(
            [
                lax.ppermute(tail, axis, [(i, (i + 1) % count) for i in range(ends)]),
                cells,
                lax.ppermute(head, axis, [((i + 1) % count, i) for i in range(ends)]),
            ],
            axis=dim,
        )
    return cells


def derivatives(padded, sx, sy, sz):

    def part(dx, dy, dz):
        return padded[:, 4 + dx : 4 + dx + sx, 4 + dy : 4 + dy + sy, 4 + dz : 4 + dz + sz]

    centre = part(0, 0, 0)
    dxx = second_coef[0] * centre
    dyy = second_coef[0] * centre
    dzz = second_coef[0] * centre
    for k in range(1, 5):
        dxx = dxx + second_coef[k] * (part(k, 0, 0) + part(-k, 0, 0))
        dyy = dyy + second_coef[k] * (part(0, k, 0) + part(0, -k, 0))
        dzz = dzz + second_coef[k] * (part(0, 0, k) + part(0, 0, -k))
    dy_wide = 0.0
    dz_xwide = 0.0
    dz_ywide = 0.0
    for k in range(1, 5):
        weight = first_coef[k - 1]
        dy_wide = dy_wide + weight * (
            padded[:, :, 4 + k : 4 + k + sy, 4 : 4 + sz]
            - padded[:, :, 4 - k : 4 - k + sy, 4 : 4 + sz]
        )
        dz_xwide = dz_xwide + weight * (
            padded[:, :, 4 : 4 + sy, 4 + k : 4 + k + sz]
            - padded[:, :, 4 : 4 + sy, 4 - k : 4 - k + sz]
        )
        dz_ywide = dz_ywide + weight * (
            padded[:, 4 : 4 + sx, :, 4 + k : 4 + k + sz]
            - padded[:, 4 : 4 + sx, :, 4 - k : 4 - k + sz]
        )
    dxy = 0.0
    dxz = 0.0
    dyz = 0.0
    for k in range(1, 5):
        weight = first_coef[k - 1]
        dxy = dxy + weight * (dy_wide[:, 4 + k : 4 + k + sx] - dy_wide[:, 4 - k : 4 - k + sx])
        dxz = dxz + weight * (dz_xwide[:, 4 + k : 4 + k + sx] - dz_xwide[:, 4 - k : 4 - k + sx])
        dyz = dyz + weight * (
            dz_ywide[:, :, 4 + k : 4 + k + sy] - dz_ywide[:, :, 4 - k : 4 - k + sy]
        )
    return (centre, dxx, dyy, dzz, dxy, dxz, dyz)


def coefficients(epsilon, delta, theta, phi):
    axis_x = jnp.sin(theta) * jnp.cos(phi)
    axis_y = jnp.sin(theta) * jnp.sin(phi)
    axis_z = jnp.cos(theta)
    return (
        axis_x * axis_x,
        axis_y * axis_y,
        axis_z * axis_z,
        2.0 * axis_x * axis_y,
        2.0 * axis_x * axis_z,
        2.0 * axis_y * axis_z,
        1.0 + 2.0 * epsilon,
        jnp.sqrt(1.0 + 2.0 * delta),
    )


def advance(padded, previous, speed, coefs, source):
    sx, sy, sz = (previous.shape[1], previous.shape[2], previous.shape[3])
    centre, dxx, dyy, dzz, dxy, dxz, dyz = derivatives(padded, sx, sy, sz)
    nxx, nyy, nzz, nxy, nxz, nyz, stretch, root_delta = coefs
    rotated = nxx * dxx + nyy * dyy + nzz * dzz + nxy * dxy + nxz * dxz + nyz * dyz
    remainder = dxx + dyy + dzz - rotated
    p_new = (
        2.0 * centre[0]
        - previous[0]
        + speed * (stretch * remainder[0] + root_delta * rotated[1])
        + source
    )
    q_new = (
        2.0 * centre[1] - previous[1] + speed * (root_delta * remainder[0] + rotated[1]) + source
    )
    return jnp.stack([p_new, q_new])


def pad_depth(fields):
    return jnp.pad(fields, ((0, 0), (0, 0), (0, 0), (4, 4)))


def from_neighbours(low_part, high_part, axis):
    count = lax.axis_size(axis)
    below = lax.ppermute(low_part, axis, [(i, i + 1) for i in range(count - 1)])
    above = lax.ppermute(high_part, axis, [(i + 1, i) for i in range(count - 1)])
    return below, above


def gather_column(traces, time_steps, rec_owner, rec_local, block):
    groups = lax.axis_size("gx")
    held = rec_local.shape[0]
    steps = jnp.arange(traces.shape[0], dtype=jnp.int32)
    chosen = (time_steps[:, None] == steps[None, :]).astype(jnp.float32)
    samples = jnp.dot(
        chosen, traces, precision=lax.Precision.HIGHEST, preferred_element_type=jnp.float32
    )
    assert groups * block < 2**24
    code = (rec_owner[:, 0] * block + rec_local).astype(jnp.float32)
    payload = jnp.concatenate([samples, code[None]])
    if groups & (groups - 1) == 0:
        arrived = payload
        step = 1
        while step < groups:
            partner = lax.ppermute(arrived, "gx", [(i, i ^ step) for i in range(groups)])
            arrived = jnp.concatenate([arrived, partner], axis=1)
            step *= 2
        return arrived
    sent = jnp.broadcast_to(payload[None], (groups, 3, held))
    arrived = lax.all_to_all(sent, "gx", split_axis=0, concat_axis=0, tiled=True)
    return jnp.transpose(arrived, (1, 0, 2)).reshape(3, groups * held)


def sources_over(arrived, values, shape, first, rows):
    sx, sy, sz = shape
    code = arrived[2].astype(jnp.int32)
    cell = code % (sx * sy * sz)
    owner = code // (sx * sy * sz)
    row = (owner - lax.axis_index("gx")) * sx + cell // (sy * sz) - first
    inside = (row >= 0) & (row < rows)
    plane = jnp.where(inside, row * sy + cell // sz % sy, -1)
    depth = cell % sz
    picks = (plane[None, :] == jnp.arange(rows * sy, dtype=jnp.int32)[:, None]).astype(jnp.float32)
    spread = values[:, None, :] * picks[None, :, :]
    columns = (depth[:, None] == jnp.arange(sz, dtype=jnp.int32)[None, :]).astype(jnp.float32)
    sources = jnp.einsum(
        "cpr,rz->cpz", spread, columns, precision=lax.Precision.HIGHEST,
        preferred_element_type=jnp.float32,
    )
    return sources.reshape(values.shape[0], rows, sy, sz)


def local(
    p_now,
    q_now,
    p_prev,
    q_prev,
    speed,
    epsilon,
    delta,
    theta,
    phi,
    snapshots,
    traces,
    time_steps,
    rec_owner,
    rec_local,
):
    sx, sy, sz = p_now.shape
    assert sx == 8
    current = jnp.stack([p_now, q_now])
    earlier = jnp.stack([p_prev, q_prev])
    params = (speed, epsilon, delta, theta, phi)

    def slabs(parts):
        return jnp.concatenate([part.reshape(-1, sy, sz) for part in parts], axis=0)

    low_part = slabs(
        [p_now, q_now, p_prev[sx - 4 :], q_prev[sx - 4 :]] + [f[sx - 4 :] for f in params]
    )
    high_part = slabs([p_now, q_now, p_prev[:4], q_prev[:4]] + [f[:4] for f in params])
    below, above = from_neighbours(low_part, high_part, "gx")

    def unpack(got):
        return (
            got[0:16].reshape(2, 8, sy, sz),
            got[16:24].reshape(2, 4, sy, sz),
            got[24:44].reshape(5, 4, sy, sz),
        )

    (now_lo, prev_lo, params_lo), (now_hi, prev_hi, params_hi) = unpack(below), unpack(above)
    now_x = jnp.concatenate([now_lo, current, now_hi], axis=1)
    prev_x = jnp.concatenate([prev_lo, earlier, prev_hi], axis=1)
    coefs = coefficients(epsilon, delta, theta, phi)
    coefs_lo = coefficients(*params_lo[1:5])
    coefs_hi = coefficients(*params_hi[1:5])
    coefs_x = [jnp.concatenate(parts, axis=0) for parts in zip(coefs_lo, coefs, coefs_hi)]
    speed_x = jnp.concatenate([params_lo[0], speed, params_hi[0]], axis=0)
    lo_y, hi_y = from_neighbours(now_x[:, :, sy - 4 :], now_x[:, :, :4], "gy")
    now_xy = pad_depth(jnp.concatenate([lo_y, now_x, hi_y], axis=2))

    arrived = gather_column(traces, time_steps, rec_owner, rec_local, sx * sy * sz)
    source_0 = sources_over(arrived, arrived[0:1], (sx, sy, sz), -4, sx + 8)[0]
    source_1 = sources_over(arrived, arrived[1:2], (sx, sy, sz), 0, sx)[0]

    mid_x = advance(now_xy, prev_x, speed_x, coefs_x, source_0)
    middle = mid_x[:, 4 : 4 + sx]
    lo_m, hi_m = from_neighbours(mid_x[:, :, sy - 4 :], mid_x[:, :, :4], "gy")
    mid_xy = pad_depth(jnp.concatenate([lo_m, mid_x, hi_m], axis=2))
    final = advance(mid_xy, current, speed, coefs, source_1)
    image = (
        snapshots[0].astype(jnp.float32) * middle[0] + snapshots[1].astype(jnp.float32) * final[0]
    )
    return (final[0], final[1], middle[0], middle[1], image)


def solution(mesh):
    return jax.shard_map(
        local,
        mesh=mesh,
        in_specs=(
            P(("shots", "gx"), "gy", None),
            P(("shots", "gx"), "gy", None),
            P(("shots", "gx"), "gy", None),
            P(("shots", "gx"), "gy", None),
            P("gx", "gy", None),
            P("gx", "gy", None),
            P("gx", "gy", None),
            P("gx", "gy", None),
            P("gx", "gy", None),
            P(None, ("shots", "gx"), "gy", None),
            P(None, ("shots", "gx", "gy")),
            P("shots"),
            P(("shots", "gx", "gy"), None),
            P(("shots", "gx", "gy")),
        ),
        out_specs=(
            P(("shots", "gx"), "gy", None),
            P(("shots", "gx"), "gy", None),
            P(("shots", "gx"), "gy", None),
            P(("shots", "gx"), "gy", None),
            P(("shots", "gx"), "gy", None),
        ),
        check_vma=False,
    )
```

```python
import jax
import jax.numpy as jnp
from jax import lax
from jax.sharding import PartitionSpec as P

second_coef = (-205.0 / 72.0, 8.0 / 5.0, -1.0 / 5.0, 8.0 / 315.0, -1.0 / 560.0)
first_coef = (4.0 / 5.0, -1.0 / 5.0, 4.0 / 105.0, -1.0 / 280.0)


def padded_2(cells, sides, width):
    for axis, dim in sides:
        count = lax.axis_size(axis)
        ends = count - 1
        head = lax.slice_in_dim(cells, 0, width, axis=dim)
        tail = lax.slice_in_dim(cells, cells.shape[dim] - width, cells.shape[dim], axis=dim)
        cells = jnp.concatenate(
            [
                lax.ppermute(tail, axis, [(i, (i + 1) % count) for i in range(ends)]),
                cells,
                lax.ppermute(head, axis, [((i + 1) % count, i) for i in range(ends)]),
            ],
            axis=dim,
        )
    return cells


def derivatives(padded, sx, sy, sz):

    def part(dx, dy, dz):
        return padded[:, 4 + dx : 4 + dx + sx, 4 + dy : 4 + dy + sy, 4 + dz : 4 + dz + sz]

    centre = part(0, 0, 0)
    dxx = second_coef[0] * centre
    dyy = second_coef[0] * centre
    dzz = second_coef[0] * centre
    for k in range(1, 5):
        dxx = dxx + second_coef[k] * (part(k, 0, 0) + part(-k, 0, 0))
        dyy = dyy + second_coef[k] * (part(0, k, 0) + part(0, -k, 0))
        dzz = dzz + second_coef[k] * (part(0, 0, k) + part(0, 0, -k))
    dy_wide = 0.0
    dz_xwide = 0.0
    dz_ywide = 0.0
    for k in range(1, 5):
        weight = first_coef[k - 1]
        dy_wide = dy_wide + weight * (
            padded[:, :, 4 + k : 4 + k + sy, 4 : 4 + sz]
            - padded[:, :, 4 - k : 4 - k + sy, 4 : 4 + sz]
        )
        dz_xwide = dz_xwide + weight * (
            padded[:, :, 4 : 4 + sy, 4 + k : 4 + k + sz]
            - padded[:, :, 4 : 4 + sy, 4 - k : 4 - k + sz]
        )
        dz_ywide = dz_ywide + weight * (
            padded[:, 4 : 4 + sx, :, 4 + k : 4 + k + sz]
            - padded[:, 4 : 4 + sx, :, 4 - k : 4 - k + sz]
        )
    dxy = 0.0
    dxz = 0.0
    dyz = 0.0
    for k in range(1, 5):
        weight = first_coef[k - 1]
        dxy = dxy + weight * (dy_wide[:, 4 + k : 4 + k + sx] - dy_wide[:, 4 - k : 4 - k + sx])
        dxz = dxz + weight * (dz_xwide[:, 4 + k : 4 + k + sx] - dz_xwide[:, 4 - k : 4 - k + sx])
        dyz = dyz + weight * (
            dz_ywide[:, :, 4 + k : 4 + k + sy] - dz_ywide[:, :, 4 - k : 4 - k + sy]
        )
    return (centre, dxx, dyy, dzz, dxy, dxz, dyz)


def coefficients(epsilon, delta, theta, phi):
    axis_x = jnp.sin(theta) * jnp.cos(phi)
    axis_y = jnp.sin(theta) * jnp.sin(phi)
    axis_z = jnp.cos(theta)
    return (
        axis_x * axis_x,
        axis_y * axis_y,
        axis_z * axis_z,
        2.0 * axis_x * axis_y,
        2.0 * axis_x * axis_z,
        2.0 * axis_y * axis_z,
        1.0 + 2.0 * epsilon,
        jnp.sqrt(1.0 + 2.0 * delta),
    )


def advance(padded, previous, speed, coefs, source):
    sx, sy, sz = (previous.shape[1], previous.shape[2], previous.shape[3])
    centre, dxx, dyy, dzz, dxy, dxz, dyz = derivatives(padded, sx, sy, sz)
    nxx, nyy, nzz, nxy, nxz, nyz, stretch, root_delta = coefs
    rotated = nxx * dxx + nyy * dyy + nzz * dzz + nxy * dxy + nxz * dxz + nyz * dyz
    remainder = dxx + dyy + dzz - rotated
    p_new = (
        2.0 * centre[0]
        - previous[0]
        + speed * (stretch * remainder[0] + root_delta * rotated[1])
        + source
    )
    q_new = (
        2.0 * centre[1] - previous[1] + speed * (root_delta * remainder[0] + rotated[1]) + source
    )
    return jnp.stack([p_new, q_new])


def pad_depth(fields):
    return jnp.pad(fields, ((0, 0), (0, 0), (0, 0), (4, 4)))


def from_neighbours(low_part, high_part, axis):
    count = lax.axis_size(axis)
    below = lax.ppermute(low_part, axis, [(i, i + 1) for i in range(count - 1)])
    above = lax.ppermute(high_part, axis, [(i + 1, i) for i in range(count - 1)])
    return below, above


def gather_column(traces, time_steps, rec_owner, rec_local, block, after):
    groups = lax.axis_size("gx")
    held = rec_local.shape[0]
    steps = jnp.arange(traces.shape[0], dtype=jnp.int32)
    chosen = (time_steps[:, None] == steps[None, :]).astype(jnp.float32)
    samples = jnp.dot(
        chosen, traces, precision=lax.Precision.HIGHEST, preferred_element_type=jnp.float32
    )
    assert groups * block < 2**24
    code = (rec_owner[:, 0] * block + rec_local).astype(jnp.float32) + 0.0 * after
    payload = jnp.concatenate([samples, code[None]])
    if groups & (groups - 1) == 0:
        arrived = payload
        step = 1
        while step < groups:
            partner = lax.ppermute(arrived, "gx", [(i, i ^ step) for i in range(groups)])
            arrived = jnp.concatenate([arrived, partner], axis=1)
            step *= 2
        return arrived
    sent = jnp.broadcast_to(payload[None], (groups, 3, held))
    arrived = lax.all_to_all(sent, "gx", split_axis=0, concat_axis=0, tiled=True)
    return jnp.transpose(arrived, (1, 0, 2)).reshape(3, groups * held)


def sources_over(arrived, values, shape, first, rows):
    sx, sy, sz = shape
    code = arrived[2].astype(jnp.int32)
    cell = code % (sx * sy * sz)
    owner = code // (sx * sy * sz)
    row = (owner - lax.axis_index("gx")) * sx + cell // (sy * sz) - first
    inside = (row >= 0) & (row < rows)
    plane = jnp.where(inside, row * sy + cell // sz % sy, -1)
    depth = cell % sz
    picks = (plane[None, :] == jnp.arange(rows * sy, dtype=jnp.int32)[:, None]).astype(jnp.float32)
    spread = values[:, None, :] * picks[None, :, :]
    columns = (depth[:, None] == jnp.arange(sz, dtype=jnp.int32)[None, :]).astype(jnp.float32)
    sources = jnp.einsum(
        "cpr,rz->cpz", spread, columns, precision=lax.Precision.HIGHEST,
        preferred_element_type=jnp.float32,
    )
    return sources.reshape(values.shape[0], rows, sy, sz)


def local(
    p_now,
    q_now,
    p_prev,
    q_prev,
    speed,
    epsilon,
    delta,
    theta,
    phi,
    snapshots,
    traces,
    time_steps,
    rec_owner,
    rec_local,
):
    sx, sy, sz = p_now.shape
    assert sx == 8
    current = jnp.stack([p_now, q_now])
    earlier = jnp.stack([p_prev, q_prev])
    params = (speed, epsilon, delta, theta, phi)

    def slabs(parts):
        return jnp.concatenate([part.reshape(-1, sy, sz) for part in parts], axis=0)

    low_part = slabs(
        [p_now, q_now, p_prev[sx - 4 :], q_prev[sx - 4 :]] + [f[sx - 4 :] for f in params]
    )
    high_part = slabs([p_now, q_now, p_prev[:4], q_prev[:4]] + [f[:4] for f in params])
    low_part, high_part = lax.optimization_barrier((low_part, high_part))
    below, above = from_neighbours(low_part, high_part, "gx")

    def unpack(got):
        return (
            got[0:16].reshape(2, 8, sy, sz),
            got[16:24].reshape(2, 4, sy, sz),
            got[24:44].reshape(5, 4, sy, sz),
        )

    (now_lo, prev_lo, params_lo), (now_hi, prev_hi, params_hi) = unpack(below), unpack(above)
    now_x = jnp.concatenate([now_lo, current, now_hi], axis=1)
    prev_x = jnp.concatenate([prev_lo, earlier, prev_hi], axis=1)
    coefs = coefficients(epsilon, delta, theta, phi)
    coefs_lo = coefficients(*params_lo[1:5])
    coefs_hi = coefficients(*params_hi[1:5])
    coefs_x = [jnp.concatenate(parts, axis=0) for parts in zip(coefs_lo, coefs, coefs_hi)]
    speed_x = jnp.concatenate([params_lo[0], speed, params_hi[0]], axis=0)
    lo_y, hi_y = from_neighbours(now_x[:, :, sy - 4 :], now_x[:, :, :4], "gy")
    now_xy = pad_depth(jnp.concatenate([lo_y, now_x, hi_y], axis=2))

    arrived = gather_column(
        traces, time_steps, rec_owner, rec_local, sx * sy * sz, low_part[0, 0, 0] + high_part[0, 0, 0]
    )
    source_0 = sources_over(arrived, arrived[0:1], (sx, sy, sz), -4, sx + 8)[0]
    source_1 = sources_over(arrived, arrived[1:2], (sx, sy, sz), 0, sx)[0]

    mid_x = advance(now_xy, prev_x, speed_x, coefs_x, source_0)
    middle = mid_x[:, 4 : 4 + sx]
    lo_m, hi_m = from_neighbours(mid_x[:, :, sy - 4 :], mid_x[:, :, :4], "gy")
    mid_xy = pad_depth(jnp.concatenate([lo_m, mid_x, hi_m], axis=2))
    final = advance(mid_xy, current, speed, coefs, source_1)
    image = (
        snapshots[0].astype(jnp.float32) * middle[0] + snapshots[1].astype(jnp.float32) * final[0]
    )
    return (final[0], final[1], middle[0], middle[1], image)


def solution(mesh):
    return jax.shard_map(
        local,
        mesh=mesh,
        in_specs=(
            P(("shots", "gx"), "gy", None),
            P(("shots", "gx"), "gy", None),
            P(("shots", "gx"), "gy", None),
            P(("shots", "gx"), "gy", None),
            P("gx", "gy", None),
            P("gx", "gy", None),
            P("gx", "gy", None),
            P("gx", "gy", None),
            P("gx", "gy", None),
            P(None, ("shots", "gx"), "gy", None),
            P(None, ("shots", "gx", "gy")),
            P("shots"),
            P(("shots", "gx", "gy"), None),
            P(("shots", "gx", "gy")),
        ),
        out_specs=(
            P(("shots", "gx"), "gy", None),
            P(("shots", "gx"), "gy", None),
            P(("shots", "gx"), "gy", None),
            P(("shots", "gx"), "gy", None),
            P(("shots", "gx"), "gy", None),
        ),
        check_vma=False,
    )
```

```python
import jax
import jax.numpy as jnp
from jax import lax
from jax.sharding import PartitionSpec as P

second_coef = (-205.0 / 72.0, 8.0 / 5.0, -1.0 / 5.0, 8.0 / 315.0, -1.0 / 560.0)
first_coef = (4.0 / 5.0, -1.0 / 5.0, 4.0 / 105.0, -1.0 / 280.0)


def padded_2(cells, sides, width):
    for axis, dim in sides:
        count = lax.axis_size(axis)
        ends = count - 1
        head = lax.slice_in_dim(cells, 0, width, axis=dim)
        tail = lax.slice_in_dim(cells, cells.shape[dim] - width, cells.shape[dim], axis=dim)
        cells = jnp.concatenate(
            [
                lax.ppermute(tail, axis, [(i, (i + 1) % count) for i in range(ends)]),
                cells,
                lax.ppermute(head, axis, [((i + 1) % count, i) for i in range(ends)]),
            ],
            axis=dim,
        )
    return cells


def derivatives(padded, sx, sy, sz):

    def part(dx, dy, dz):
        return padded[:, 4 + dx : 4 + dx + sx, 4 + dy : 4 + dy + sy, 4 + dz : 4 + dz + sz]

    centre = part(0, 0, 0)
    dxx = second_coef[0] * centre
    dyy = second_coef[0] * centre
    dzz = second_coef[0] * centre
    for k in range(1, 5):
        dxx = dxx + second_coef[k] * (part(k, 0, 0) + part(-k, 0, 0))
        dyy = dyy + second_coef[k] * (part(0, k, 0) + part(0, -k, 0))
        dzz = dzz + second_coef[k] * (part(0, 0, k) + part(0, 0, -k))
    dy_wide = 0.0
    dz_xwide = 0.0
    dz_ywide = 0.0
    for k in range(1, 5):
        weight = first_coef[k - 1]
        dy_wide = dy_wide + weight * (
            padded[:, :, 4 + k : 4 + k + sy, 4 : 4 + sz]
            - padded[:, :, 4 - k : 4 - k + sy, 4 : 4 + sz]
        )
        dz_xwide = dz_xwide + weight * (
            padded[:, :, 4 : 4 + sy, 4 + k : 4 + k + sz]
            - padded[:, :, 4 : 4 + sy, 4 - k : 4 - k + sz]
        )
        dz_ywide = dz_ywide + weight * (
            padded[:, 4 : 4 + sx, :, 4 + k : 4 + k + sz]
            - padded[:, 4 : 4 + sx, :, 4 - k : 4 - k + sz]
        )
    dxy = 0.0
    dxz = 0.0
    dyz = 0.0
    for k in range(1, 5):
        weight = first_coef[k - 1]
        dxy = dxy + weight * (dy_wide[:, 4 + k : 4 + k + sx] - dy_wide[:, 4 - k : 4 - k + sx])
        dxz = dxz + weight * (dz_xwide[:, 4 + k : 4 + k + sx] - dz_xwide[:, 4 - k : 4 - k + sx])
        dyz = dyz + weight * (
            dz_ywide[:, :, 4 + k : 4 + k + sy] - dz_ywide[:, :, 4 - k : 4 - k + sy]
        )
    return (centre, dxx, dyy, dzz, dxy, dxz, dyz)


def coefficients(epsilon, delta, theta, phi):
    axis_x = jnp.sin(theta) * jnp.cos(phi)
    axis_y = jnp.sin(theta) * jnp.sin(phi)
    axis_z = jnp.cos(theta)
    return (
        axis_x * axis_x,
        axis_y * axis_y,
        axis_z * axis_z,
        2.0 * axis_x * axis_y,
        2.0 * axis_x * axis_z,
        2.0 * axis_y * axis_z,
        1.0 + 2.0 * epsilon,
        jnp.sqrt(1.0 + 2.0 * delta),
    )


def advance(padded, previous, speed, coefs, source):
    sx, sy, sz = (previous.shape[1], previous.shape[2], previous.shape[3])
    centre, dxx, dyy, dzz, dxy, dxz, dyz = derivatives(padded, sx, sy, sz)
    nxx, nyy, nzz, nxy, nxz, nyz, stretch, root_delta = coefs
    rotated = nxx * dxx + nyy * dyy + nzz * dzz + nxy * dxy + nxz * dxz + nyz * dyz
    remainder = dxx + dyy + dzz - rotated
    p_new = (
        2.0 * centre[0]
        - previous[0]
        + speed * (stretch * remainder[0] + root_delta * rotated[1])
        + source
    )
    q_new = (
        2.0 * centre[1] - previous[1] + speed * (root_delta * remainder[0] + rotated[1]) + source
    )
    return jnp.stack([p_new, q_new])


def pad_depth(fields):
    return jnp.pad(fields, ((0, 0), (0, 0), (0, 0), (4, 4)))


def from_neighbours(low_part, high_part, axis):
    count = lax.axis_size(axis)
    below = lax.ppermute(low_part, axis, [(i, i + 1) for i in range(count - 1)])
    above = lax.ppermute(high_part, axis, [(i + 1, i) for i in range(count - 1)])
    return below, above


def gather_column(traces, time_steps, rec_owner, rec_local, block):
    groups = lax.axis_size("gx")
    held = rec_local.shape[0]
    steps = jnp.arange(traces.shape[0], dtype=jnp.int32)
    chosen = (time_steps[:, None] == steps[None, :]).astype(jnp.float32)
    samples = jnp.dot(
        chosen, traces, precision=lax.Precision.HIGHEST, preferred_element_type=jnp.float32
    )
    assert groups * block < 2**24
    code = (rec_owner[:, 0] * block + rec_local).astype(jnp.float32)
    payload = jnp.concatenate([samples, code[None]])
    if groups & (groups - 1) == 0:
        arrived = payload
        step = groups // 2
        while step >= 1:
            partner = lax.ppermute(arrived, "gx", [(i, i ^ step) for i in range(groups)])
            arrived = jnp.concatenate([arrived, partner], axis=1)
            step //= 2
        return arrived
    sent = jnp.broadcast_to(payload[None], (groups, 3, held))
    arrived = lax.all_to_all(sent, "gx", split_axis=0, concat_axis=0, tiled=True)
    return jnp.transpose(arrived, (1, 0, 2)).reshape(3, groups * held)


def sources_over(arrived, values, shape, first, rows):
    sx, sy, sz = shape
    code = arrived[2].astype(jnp.int32)
    cell = code % (sx * sy * sz)
    owner = code // (sx * sy * sz)
    row = (owner - lax.axis_index("gx")) * sx + cell // (sy * sz) - first
    inside = (row >= 0) & (row < rows)
    plane = jnp.where(inside, row * sy + cell // sz % sy, -1)
    depth = cell % sz
    picks = (plane[None, :] == jnp.arange(rows * sy, dtype=jnp.int32)[:, None]).astype(jnp.float32)
    spread = values[:, None, :] * picks[None, :, :]
    columns = (depth[:, None] == jnp.arange(sz, dtype=jnp.int32)[None, :]).astype(jnp.float32)
    sources = jnp.einsum(
        "cpr,rz->cpz", spread, columns, precision=lax.Precision.HIGHEST,
        preferred_element_type=jnp.float32,
    )
    return sources.reshape(values.shape[0], rows, sy, sz)


def local(
    p_now,
    q_now,
    p_prev,
    q_prev,
    speed,
    epsilon,
    delta,
    theta,
    phi,
    snapshots,
    traces,
    time_steps,
    rec_owner,
    rec_local,
):
    sx, sy, sz = p_now.shape
    assert sx == 8
    current = jnp.stack([p_now, q_now])
    earlier = jnp.stack([p_prev, q_prev])
    params = (speed, epsilon, delta, theta, phi)

    def slabs(parts):
        return jnp.concatenate([part.reshape(-1, sy, sz) for part in parts], axis=0)

    low_part = slabs(
        [p_now, q_now, p_prev[sx - 4 :], q_prev[sx - 4 :]] + [f[sx - 4 :] for f in params]
    )
    high_part = slabs([p_now, q_now, p_prev[:4], q_prev[:4]] + [f[:4] for f in params])
    below, above = from_neighbours(low_part, high_part, "gx")

    def unpack(got):
        return (
            got[0:16].reshape(2, 8, sy, sz),
            got[16:24].reshape(2, 4, sy, sz),
            got[24:44].reshape(5, 4, sy, sz),
        )

    (now_lo, prev_lo, params_lo), (now_hi, prev_hi, params_hi) = unpack(below), unpack(above)
    now_x = jnp.concatenate([now_lo, current, now_hi], axis=1)
    prev_x = jnp.concatenate([prev_lo, earlier, prev_hi], axis=1)
    coefs = coefficients(epsilon, delta, theta, phi)
    coefs_lo = coefficients(*params_lo[1:5])
    coefs_hi = coefficients(*params_hi[1:5])
    coefs_x = [jnp.concatenate(parts, axis=0) for parts in zip(coefs_lo, coefs, coefs_hi)]
    speed_x = jnp.concatenate([params_lo[0], speed, params_hi[0]], axis=0)
    lo_y, hi_y = from_neighbours(now_x[:, :, sy - 4 :], now_x[:, :, :4], "gy")
    now_xy = pad_depth(jnp.concatenate([lo_y, now_x, hi_y], axis=2))

    arrived = gather_column(traces, time_steps, rec_owner, rec_local, sx * sy * sz)
    source_0 = sources_over(arrived, arrived[0:1], (sx, sy, sz), -4, sx + 8)[0]
    source_1 = sources_over(arrived, arrived[1:2], (sx, sy, sz), 0, sx)[0]

    mid_x = advance(now_xy, prev_x, speed_x, coefs_x, source_0)
    middle = mid_x[:, 4 : 4 + sx]
    lo_m, hi_m = from_neighbours(mid_x[:, :, sy - 4 :], mid_x[:, :, :4], "gy")
    mid_xy = pad_depth(jnp.concatenate([lo_m, mid_x, hi_m], axis=2))
    final = advance(mid_xy, current, speed, coefs, source_1)
    image = (
        snapshots[0].astype(jnp.float32) * middle[0] + snapshots[1].astype(jnp.float32) * final[0]
    )
    return (final[0], final[1], middle[0], middle[1], image)


def solution(mesh):
    return jax.shard_map(
        local,
        mesh=mesh,
        in_specs=(
            P(("shots", "gx"), "gy", None),
            P(("shots", "gx"), "gy", None),
            P(("shots", "gx"), "gy", None),
            P(("shots", "gx"), "gy", None),
            P("gx", "gy", None),
            P("gx", "gy", None),
            P("gx", "gy", None),
            P("gx", "gy", None),
            P("gx", "gy", None),
            P(None, ("shots", "gx"), "gy", None),
            P(None, ("shots", "gx", "gy")),
            P("shots"),
            P(("shots", "gx", "gy"), None),
            P(("shots", "gx", "gy")),
        ),
        out_specs=(
            P(("shots", "gx"), "gy", None),
            P(("shots", "gx"), "gy", None),
            P(("shots", "gx"), "gy", None),
            P(("shots", "gx"), "gy", None),
            P(("shots", "gx"), "gy", None),
        ),
        check_vma=False,
    )
```

```python
import jax
import jax.numpy as jnp
from jax import lax
from jax.sharding import PartitionSpec as P

second_coef = (-205.0 / 72.0, 8.0 / 5.0, -1.0 / 5.0, 8.0 / 315.0, -1.0 / 560.0)
first_coef = (4.0 / 5.0, -1.0 / 5.0, 4.0 / 105.0, -1.0 / 280.0)


def padded_2(cells, sides, width):
    for axis, dim in sides:
        count = lax.axis_size(axis)
        ends = count - 1
        head = lax.slice_in_dim(cells, 0, width, axis=dim)
        tail = lax.slice_in_dim(cells, cells.shape[dim] - width, cells.shape[dim], axis=dim)
        cells = jnp.concatenate(
            [
                lax.ppermute(tail, axis, [(i, (i + 1) % count) for i in range(ends)]),
                cells,
                lax.ppermute(head, axis, [((i + 1) % count, i) for i in range(ends)]),
            ],
            axis=dim,
        )
    return cells


def derivatives(padded, sx, sy, sz):

    def part(dx, dy, dz):
        return padded[:, 4 + dx : 4 + dx + sx, 4 + dy : 4 + dy + sy, 4 + dz : 4 + dz + sz]

    centre = part(0, 0, 0)
    dxx = second_coef[0] * centre
    dyy = second_coef[0] * centre
    dzz = second_coef[0] * centre
    for k in range(1, 5):
        dxx = dxx + second_coef[k] * (part(k, 0, 0) + part(-k, 0, 0))
        dyy = dyy + second_coef[k] * (part(0, k, 0) + part(0, -k, 0))
        dzz = dzz + second_coef[k] * (part(0, 0, k) + part(0, 0, -k))
    dy_wide = 0.0
    dz_xwide = 0.0
    dz_ywide = 0.0
    for k in range(1, 5):
        weight = first_coef[k - 1]
        dy_wide = dy_wide + weight * (
            padded[:, :, 4 + k : 4 + k + sy, 4 : 4 + sz]
            - padded[:, :, 4 - k : 4 - k + sy, 4 : 4 + sz]
        )
        dz_xwide = dz_xwide + weight * (
            padded[:, :, 4 : 4 + sy, 4 + k : 4 + k + sz]
            - padded[:, :, 4 : 4 + sy, 4 - k : 4 - k + sz]
        )
        dz_ywide = dz_ywide + weight * (
            padded[:, 4 : 4 + sx, :, 4 + k : 4 + k + sz]
            - padded[:, 4 : 4 + sx, :, 4 - k : 4 - k + sz]
        )
    dxy = 0.0
    dxz = 0.0
    dyz = 0.0
    for k in range(1, 5):
        weight = first_coef[k - 1]
        dxy = dxy + weight * (dy_wide[:, 4 + k : 4 + k + sx] - dy_wide[:, 4 - k : 4 - k + sx])
        dxz = dxz + weight * (dz_xwide[:, 4 + k : 4 + k + sx] - dz_xwide[:, 4 - k : 4 - k + sx])
        dyz = dyz + weight * (
            dz_ywide[:, :, 4 + k : 4 + k + sy] - dz_ywide[:, :, 4 - k : 4 - k + sy]
        )
    return (centre, dxx, dyy, dzz, dxy, dxz, dyz)


def coefficients(epsilon, delta, theta, phi):
    axis_x = jnp.sin(theta) * jnp.cos(phi)
    axis_y = jnp.sin(theta) * jnp.sin(phi)
    axis_z = jnp.cos(theta)
    return (
        axis_x * axis_x,
        axis_y * axis_y,
        axis_z * axis_z,
        2.0 * axis_x * axis_y,
        2.0 * axis_x * axis_z,
        2.0 * axis_y * axis_z,
        1.0 + 2.0 * epsilon,
        jnp.sqrt(1.0 + 2.0 * delta),
    )


def advance(padded, previous, speed, coefs, source):
    sx, sy, sz = (previous.shape[1], previous.shape[2], previous.shape[3])
    centre, dxx, dyy, dzz, dxy, dxz, dyz = derivatives(padded, sx, sy, sz)
    nxx, nyy, nzz, nxy, nxz, nyz, stretch, root_delta = coefs
    rotated = nxx * dxx + nyy * dyy + nzz * dzz + nxy * dxy + nxz * dxz + nyz * dyz
    remainder = dxx + dyy + dzz - rotated
    p_new = (
        2.0 * centre[0]
        - previous[0]
        + speed * (stretch * remainder[0] + root_delta * rotated[1])
        + source
    )
    q_new = (
        2.0 * centre[1] - previous[1] + speed * (root_delta * remainder[0] + rotated[1]) + source
    )
    return jnp.stack([p_new, q_new])


def pad_depth(fields):
    return jnp.pad(fields, ((0, 0), (0, 0), (0, 0), (4, 4)))


def from_neighbours(low_part, high_part, axis):
    count = lax.axis_size(axis)
    below = lax.ppermute(low_part, axis, [(i, i + 1) for i in range(count - 1)])
    above = lax.ppermute(high_part, axis, [(i + 1, i) for i in range(count - 1)])
    return below, above


def gather_column(traces, time_steps, rec_owner, rec_local, block):
    groups = lax.axis_size("gx")
    held = rec_local.shape[0]
    steps = jnp.arange(traces.shape[0], dtype=jnp.int32)
    chosen = (time_steps[:, None] == steps[None, :]).astype(jnp.float32)
    samples = jnp.dot(
        chosen, traces, precision=lax.Precision.HIGH, preferred_element_type=jnp.float32
    )
    assert groups * block < 2**24
    code = (rec_owner[:, 0] * block + rec_local).astype(jnp.float32)
    payload = jnp.concatenate([samples, code[None]])
    if groups & (groups - 1) == 0:
        arrived = payload
        step = 1
        while step < groups:
            partner = lax.ppermute(arrived, "gx", [(i, i ^ step) for i in range(groups)])
            arrived = jnp.concatenate([arrived, partner], axis=1)
            step *= 2
        return arrived
    sent = jnp.broadcast_to(payload[None], (groups, 3, held))
    arrived = lax.all_to_all(sent, "gx", split_axis=0, concat_axis=0, tiled=True)
    return jnp.transpose(arrived, (1, 0, 2)).reshape(3, groups * held)


def sources_over(arrived, values, shape, first, rows):
    sx, sy, sz = shape
    code = arrived[2].astype(jnp.int32)
    cell = code % (sx * sy * sz)
    owner = code // (sx * sy * sz)
    row = (owner - lax.axis_index("gx")) * sx + cell // (sy * sz) - first
    inside = (row >= 0) & (row < rows)
    plane = jnp.where(inside, row * sy + cell // sz % sy, -1)
    depth = cell % sz
    picks = (plane[None, :] == jnp.arange(rows * sy, dtype=jnp.int32)[:, None]).astype(jnp.float32)
    spread = values[:, None, :] * picks[None, :, :]
    columns = (depth[:, None] == jnp.arange(sz, dtype=jnp.int32)[None, :]).astype(jnp.float32)
    sources = jnp.einsum(
        "cpr,rz->cpz", spread, columns, precision=lax.Precision.HIGH,
        preferred_element_type=jnp.float32,
    )
    return sources.reshape(values.shape[0], rows, sy, sz)


def local(
    p_now,
    q_now,
    p_prev,
    q_prev,
    speed,
    epsilon,
    delta,
    theta,
    phi,
    snapshots,
    traces,
    time_steps,
    rec_owner,
    rec_local,
):
    sx, sy, sz = p_now.shape
    assert sx == 8
    current = jnp.stack([p_now, q_now])
    earlier = jnp.stack([p_prev, q_prev])
    params = (speed, epsilon, delta, theta, phi)

    def slabs(parts):
        return jnp.concatenate([part.reshape(-1, sy, sz) for part in parts], axis=0)

    low_part = slabs(
        [p_now, q_now, p_prev[sx - 4 :], q_prev[sx - 4 :]] + [f[sx - 4 :] for f in params]
    )
    high_part = slabs([p_now, q_now, p_prev[:4], q_prev[:4]] + [f[:4] for f in params])
    below, above = from_neighbours(low_part, high_part, "gx")

    def unpack(got):
        return (
            got[0:16].reshape(2, 8, sy, sz),
            got[16:24].reshape(2, 4, sy, sz),
            got[24:44].reshape(5, 4, sy, sz),
        )

    (now_lo, prev_lo, params_lo), (now_hi, prev_hi, params_hi) = unpack(below), unpack(above)
    now_x = jnp.concatenate([now_lo, current, now_hi], axis=1)
    prev_x = jnp.concatenate([prev_lo, earlier, prev_hi], axis=1)
    coefs = coefficients(epsilon, delta, theta, phi)
    coefs_lo = coefficients(*params_lo[1:5])
    coefs_hi = coefficients(*params_hi[1:5])
    coefs_x = [jnp.concatenate(parts, axis=0) for parts in zip(coefs_lo, coefs, coefs_hi)]
    speed_x = jnp.concatenate([params_lo[0], speed, params_hi[0]], axis=0)
    lo_y, hi_y = from_neighbours(now_x[:, :, sy - 4 :], now_x[:, :, :4], "gy")
    now_xy = pad_depth(jnp.concatenate([lo_y, now_x, hi_y], axis=2))

    arrived = gather_column(traces, time_steps, rec_owner, rec_local, sx * sy * sz)
    source_0 = sources_over(arrived, arrived[0:1], (sx, sy, sz), -4, sx + 8)[0]
    source_1 = sources_over(arrived, arrived[1:2], (sx, sy, sz), 0, sx)[0]

    mid_x = advance(now_xy, prev_x, speed_x, coefs_x, source_0)
    middle = mid_x[:, 4 : 4 + sx]
    lo_m, hi_m = from_neighbours(mid_x[:, :, sy - 4 :], mid_x[:, :, :4], "gy")
    mid_xy = pad_depth(jnp.concatenate([lo_m, mid_x, hi_m], axis=2))
    final = advance(mid_xy, current, speed, coefs, source_1)
    image = (
        snapshots[0].astype(jnp.float32) * middle[0] + snapshots[1].astype(jnp.float32) * final[0]
    )
    return (final[0], final[1], middle[0], middle[1], image)


def solution(mesh):
    return jax.shard_map(
        local,
        mesh=mesh,
        in_specs=(
            P(("shots", "gx"), "gy", None),
            P(("shots", "gx"), "gy", None),
            P(("shots", "gx"), "gy", None),
            P(("shots", "gx"), "gy", None),
            P("gx", "gy", None),
            P("gx", "gy", None),
            P("gx", "gy", None),
            P("gx", "gy", None),
            P("gx", "gy", None),
            P(None, ("shots", "gx"), "gy", None),
            P(None, ("shots", "gx", "gy")),
            P("shots"),
            P(("shots", "gx", "gy"), None),
            P(("shots", "gx", "gy")),
        ),
        out_specs=(
            P(("shots", "gx"), "gy", None),
            P(("shots", "gx"), "gy", None),
            P(("shots", "gx"), "gy", None),
            P(("shots", "gx"), "gy", None),
            P(("shots", "gx"), "gy", None),
        ),
        check_vma=False,
    )
```
